512 devices in a mesh: lat: 16 (over z_hi, x, core), lon: 32 (over z_lo, y).
Axes of the slice: x: 4, y: 8, z: 8 (z_hi: 2, z_lo: 4; z = z_hi * 4 + z_lo), core: 2. Of those that a mesh axis runs over, the one named last changes fastest.
Arguments:
- field: bfloat16 [64, 4096, 512], P('lat', 'lon'), may hold values from -6 to 6
- lon_width: int32 [64], P('lat'), may hold values from 1 to 256, as said below
- lon_taps: float32 [64, 9, 513], P('lat'), may hold values from -0.375 to 0.375
- row_scale: float32 [64], P('lat'), may hold values from 0.05 to 0.2
- support: int32 [1536, 3], P('lat'), may hold values from -2 to 8, as said below
- mix_weight: bfloat16 [9, 512, 512], replicated, may hold values from -0.25 to 0.25
Outputs:
- block_out: bfloat16 [64, 4096, 512], P('lat', 'lon')
The draws below stay inside these ranges and needn't reach their ends.
Inputs may be any that keep to these rules, and one draw needn't show every extreme that they name: `lon_width`: the first row of the slab has a half-width of 256. `support`: the output row lies in the entry's band, the input row within 2 rows of it; every output row has 24 entries, stored in order of output row.
All inputs are finite; a program needn't handle non-finite values.
Results may differ from the reference program's by a relative error of at most 0.0057.
Values may be sent and summed in bfloat16 or wider, within the bound.
No kernel may reach another device: no remote copies, remote signals or barrier semaphores. Data moves between devices by JAX's collectives and lax.ppermute only.
A program may use at most 192 MiB of HBM per device.

```python
import math
import jax
import jax.numpy as jnp
from jax import lax

C = 512
K = 9
LAT_DEV = 4
RIM = 2
NPER = 24
HMAX = 256
TAPS = 513
SUP_DEV = 96
LAT = 64
LON = 4096
SUP = 1536


def draw_lon_width(key, part):
    rows = jnp.arange(LAT, dtype=jnp.int32)
    spread = max(1, LAT // 8)
    base = HMAX * spread // (rows + spread)
    jitter = jax.random.randint(key, (LAT,), 0, 8, dtype=jnp.int32)
    return jnp.minimum(base + jitter, HMAX).astype(jnp.int32)


def draw_support(key, part):
    bands = SUP // SUP_DEV
    first, second = jax.random.split(key)
    layout = (bands, LAT_DEV, NPER)
    delta = jax.random.randint(first, layout, -RIM, RIM + 1, dtype=jnp.int32)
    delta = delta.at[:, 0, 0].set(-RIM).at[:, LAT_DEV - 1, 0].set(RIM)
    basis = jax.random.randint(second, layout, 0, K, dtype=jnp.int32)
    basis = basis.at[:, 0, 0].set(K - 1)
    out_rows = jnp.broadcast_to(jnp.arange(LAT_DEV, dtype=jnp.int32)[None, :, None], layout)
    table = jnp.stack([out_rows, out_rows + delta, basis], axis=-1)
    return table.reshape(SUP, 3).astype(jnp.int32)


def levels(rng, shape, cuts, least, largest):
    factor_of, own = 1.0, jax.random.fold_in(rng, 6)
    for axis_at, blocks in cuts:
        steps = jnp.exp(jax.random.uniform(jax.random.fold_in(own, axis_at), (blocks,), jnp.float32, least / len(cuts), largest / len(cuts)))
        factor_of = factor_of * jnp.repeat(steps, shape[axis_at] // blocks).reshape([-1 if axis == axis_at else 1 for axis in range(len(shape))])
    return factor_of


def gaussian(key, shape, width, most, pieces=(), kind=jnp.bfloat16):
    factor_of = levels(key, shape, pieces, -0.22, 0.18) if pieces else 1.0
    drawn = jax.random.normal(key, shape, jnp.float32) * width * factor_of
    return jnp.minimum(jnp.maximum(drawn, -most), most).astype(kind)


def setup_inputs(seed: int = 0) -> dict:
    arg_keys = jax.random.split(jax.random.key(seed), 7)
    return {
        "field": gaussian(arg_keys[0], (LAT, LON, C), 1.0, 6.0, ((0, 16), (1, 32))),
        "lon_width": draw_lon_width(jax.random.fold_in(arg_keys[6], 71), 0),
        "lon_taps": gaussian(arg_keys[2], (LAT, K, TAPS), HMAX ** -0.5, 0.375, ((0, 16),), jnp.float32),
        "row_scale": jnp.clip(jnp.exp(math.log(0.2) - 1.3862944 * jax.random.uniform(arg_keys[3], (LAT,), jnp.float32) ** levels(arg_keys[3], (LAT,), ((0, 16),), -0.2, 0.2)), 0.05, 0.2),
        "support": draw_support(jax.random.fold_in(arg_keys[6], 71), 0),
        "mix_weight": gaussian(arg_keys[5], (K, C, C), C ** -0.5, 0.25),
    }


def reference(field, lon_width, lon_taps, row_scale, support, mix_weight):
    distance = jnp.abs(jnp.arange(TAPS, dtype=jnp.int32) - HMAX)
    keep = distance[None, None, :] <= lon_width[:, None, None]
    taps_masked = jnp.where(keep, lon_taps, 0.0).astype(jnp.bfloat16)
    places = (jnp.arange(TAPS, dtype=jnp.int32) - HMAX) % LON
    kernel = jnp.zeros((LAT, K, LON), jnp.float32).at[:, :, places].set(taps_masked.astype(jnp.float32))
    kernel_spectrum = jnp.conj(jnp.fft.rfft(kernel, axis=2))
    bands = jnp.arange(SUP, dtype=jnp.int32) // SUP_DEV
    out_global = bands * LAT_DEV + support[:, 0]
    in_global = bands * LAT_DEV + support[:, 1]
    valid = (in_global >= 0) & (in_global < LAT)
    slots = ((out_global * K + support[:, 2]) * (2 * RIM + 1) + (in_global - out_global + RIM)).astype(jnp.int32)
    counts = jax.ops.segment_sum(valid.astype(jnp.float32), slots, num_segments=LAT * K * (2 * RIM + 1))
    counts = counts.reshape(LAT, K, 2 * RIM + 1)
    weights = mix_weight.astype(jnp.float32)

    def one_row(row):
        picks = row - RIM + jnp.arange(2 * RIM + 1, dtype=jnp.int32)
        inside = (picks >= 0) & (picks < LAT)
        safe = jnp.clip(picks, 0, LAT - 1)
        spectrum = jnp.fft.rfft(field[safe].astype(jnp.float32), axis=1)
        product = kernel_spectrum[safe][:, :, :, None] * spectrum[:, None, :, :]
        responses = jnp.fft.irfft(product, n=LON, axis=2).astype(jnp.bfloat16)
        responses = lax.optimization_barrier(responses).astype(jnp.float32)
        factor = counts[row] * inside.astype(jnp.float32)[None, :]
        coupled = jnp.einsum("kr,rkjc->kjc", factor, responses, precision=lax.Precision.HIGHEST)
        mixed = jnp.einsum("kjc,kcd->jd", coupled, weights, precision=lax.Precision.HIGHEST)
        return (mixed * row_scale[row]).astype(jnp.bfloat16)

    return lax.map(one_row, jnp.arange(LAT, dtype=jnp.int32))
```

```python
import jax
import jax.numpy as jnp
from jax import lax
from jax.experimental import pallas as pl
from jax.experimental.pallas import tpu as pltpu
from jax.sharding import PartitionSpec as P

SPAN = 2
RIM = 2


def shifted(value, axis, by):
    length = lax.axis_size(axis)
    return lax.ppermute(value, axis, [(i, (i + by) % length) for i in range(length)])


def with_halo(block, sides, width):
    for axis, dim in sides:
        count = lax.axis_size(axis)
        forward = [(i, i + 1) for i in range(count - 1)]
        backward = [(target, source) for source, target in forward]
        low = lax.ppermute(
            lax.slice_in_dim(block, block.shape[dim] - width, None, axis=dim), axis, forward
        )
        high = lax.ppermute(lax.slice_in_dim(block, 0, width, axis=dim), axis, backward)
        block = jnp.concatenate([low, block, high], axis=dim)
    return block


def masked_taps(lon_taps, lon_width):
    length = lon_taps.shape[2]
    middle = (length - 1) // 2
    distance = jnp.abs(jnp.arange(length, dtype=jnp.int32) - middle)
    keep = distance[None, None, :] <= lon_width[:, None, None]
    return jnp.where(keep, lon_taps, 0.0).astype(jnp.bfloat16)


def _toeplitz_kernel(taps_ref, out_ref):
    kinds = taps_ref.shape[1]
    cols = out_ref.shape[2]
    for kind in range(kinds):
        row = taps_ref[0, kind : kind + 1, :]
        wide = jnp.broadcast_to(row, (cols, row.shape[1]))
        out_ref[0, kind] = pltpu.roll(wide, 0, 1, stride=1, stride_axis=0).astype(out_ref.dtype)


def band_matrix(short_taps, cols, window):
    rows, kinds, length = short_taps.shape
    padded = jnp.pad(short_taps.astype(jnp.float32), ((0, 0), (0, 0), (0, window - length)))
    return pl.pallas_call(
        _toeplitz_kernel,
        grid=(rows,),
        in_specs=[pl.BlockSpec((1, kinds, window), lambda i: (i, 0, 0))],
        out_specs=pl.BlockSpec((1, kinds, cols, window), lambda i: (i, 0, 0, 0)),
        out_shape=jax.ShapeDtypeStruct((rows, kinds, cols, window), jnp.bfloat16),
    )(padded)


def longitude_halo(source):
    west = shifted(source, "lon", 1)
    east = shifted(source, "lon", -1)
    far_west = shifted(west, "lon", 1)
    far_east = shifted(east, "lon", -1)
    return far_west, west, east, far_east


def coupling(out_rows, in_rows, basis, valid, output_rows, input_rows, kinds):
    out_match = (out_rows[:, None] == jnp.arange(output_rows, dtype=jnp.int32)[None, :]) & valid[
        :, None
    ]
    in_match = (basis * input_rows + in_rows)[:, None] == jnp.arange(
        kinds * input_rows, dtype=jnp.int32
    )[None, :]
    table = jnp.dot(
        out_match.astype(jnp.float32).T,
        in_match.astype(jnp.float32),
        precision=lax.Precision.HIGHEST,
    )
    return table.reshape(output_rows, kinds, input_rows)


def combine(counts, mixed):
    total = None
    for basis_index in range(mixed.shape[0]):
        for row in range(mixed.shape[1]):
            term = counts[:, basis_index, row][:, None, None] * mixed[basis_index, row][None]
            total = term if total is None else total + term
    return total


def on_device(field, lon_width, lon_taps, row_scale, support, mix_weight):
    rows = field.shape[0]
    cols = field.shape[1]
    kinds = lon_taps.shape[1]
    far_west, west, east, far_east = longitude_halo(field)
    short_taps = masked_taps(lon_taps, lon_width)
    window = cols * (2 * SPAN + 1)
    toeplitz = band_matrix(short_taps, cols, window)
    local = jnp.einsum(
        "ikjp,ipc->ikjc",
        toeplitz[:, :, :, SPAN * cols : (SPAN + 1) * cols],
        field,
        preferred_element_type=jnp.float32,
    )
    halo = jnp.concatenate([far_west, west, east, far_east], axis=1)
    halo_taps = jnp.concatenate(
        [toeplitz[:, :, :, : SPAN * cols], toeplitz[:, :, :, (SPAN + 1) * cols :]], axis=3
    )
    responses = (
        local + jnp.einsum("ikjp,ipc->ikjc", halo_taps, halo, preferred_element_type=jnp.float32)
    ).astype(jnp.bfloat16)
    entries = support.shape[0]
    lists = with_halo(support, (("lat", 0),), entries)
    above = lists[:entries]
    below = lists[2 * entries :]
    out_rows = jnp.concatenate(
        [support[:, 0] + RIM, above[:, 0] - rows + RIM, below[:, 0] + rows + RIM]
    )
    in_rows = jnp.concatenate([support[:, 1], above[:, 1] - rows, below[:, 1] + rows])
    basis = jnp.concatenate([support[:, 2], above[:, 2], below[:, 2]])
    valid = jnp.concatenate(
        [(support[:, 1] >= 0) & (support[:, 1] < rows), above[:, 1] >= rows, below[:, 1] < 0]
    )
    counts = coupling(out_rows, in_rows, basis, valid, rows + 2 * RIM, rows, kinds)
    mixed = jnp.einsum(
        "ikjc,kcd->kijd", responses, mix_weight, preferred_element_type=jnp.float32
    )
    edges = jnp.concatenate([counts[:RIM], counts[rows + RIM :]], axis=0)
    outgoing = combine(edges, mixed)
    incoming = with_halo(outgoing.astype(jnp.bfloat16), (("lat", 0),), RIM).astype(jnp.float32)
    inner = combine(counts[RIM : RIM + rows], mixed)
    inner = inner + jnp.pad(incoming[:RIM], ((0, rows - RIM), (0, 0), (0, 0)))
    inner = inner + jnp.pad(incoming[3 * RIM :], ((rows - RIM, 0), (0, 0), (0, 0)))
    return (inner * row_scale[:, None, None]).astype(jnp.bfloat16)


def solution(mesh):
    in_specs = (
        P("lat", "lon", None),
        P("lat"),
        P("lat", None, None),
        P("lat"),
        P("lat", None),
        P(),
    )
    out_specs = P("lat", "lon", None)
    return jax.shard_map(
        on_device, mesh=mesh, in_specs=in_specs, out_specs=out_specs, check_vma=False
    )
```

```python
import jax
import jax.numpy as jnp
from jax import lax
from jax.experimental import pallas as pl
from jax.experimental.pallas import tpu as pltpu
from jax.sharding import PartitionSpec as P

SPAN = 2
RIM = 2


def shifted(value, axis, by):
    length = lax.axis_size(axis)
    return lax.ppermute(value, axis, [(i, (i + by) % length) for i in range(length)])


def with_halo(block, sides, width):
    for axis, dim in sides:
        count = lax.axis_size(axis)
        forward = [(i, i + 1) for i in range(count - 1)]
        backward = [(target, source) for source, target in forward]
        low = lax.ppermute(
            lax.slice_in_dim(block, block.shape[dim] - width, None, axis=dim), axis, forward
        )
        high = lax.ppermute(lax.slice_in_dim(block, 0, width, axis=dim), axis, backward)
        block = jnp.concatenate([low, block, high], axis=dim)
    return block


def masked_taps(lon_taps, lon_width):
    length = lon_taps.shape[2]
    middle = (length - 1) // 2
    distance = jnp.abs(jnp.arange(length, dtype=jnp.int32) - middle)
    keep = distance[None, None, :] <= lon_width[:, None, None]
    return jnp.where(keep, lon_taps, 0.0).astype(jnp.bfloat16)


def longitude_halo(source):
    west = shifted(source, "lon", 1)
    east = shifted(source, "lon", -1)
    far_west = shifted(west, "lon", 1)
    far_east = shifted(east, "lon", -1)
    return far_west, west, east, far_east


def coupling(out_rows, in_rows, basis, valid, output_rows, input_rows, kinds):
    out_match = (out_rows[:, None] == jnp.arange(output_rows, dtype=jnp.int32)[None, :]) & valid[
        :, None
    ]
    in_match = (basis * input_rows + in_rows)[:, None] == jnp.arange(
        kinds * input_rows, dtype=jnp.int32
    )[None, :]
    table = jnp.dot(
        out_match.astype(jnp.float32).T,
        in_match.astype(jnp.float32),
        precision=lax.Precision.HIGHEST,
    )
    return table.reshape(output_rows, kinds, input_rows)


def _block_kernel(counts_ref, taps_ref, far_west_ref, west_ref, local_ref, east_ref, far_east_ref,
                  weight_ref, edge_ref, inner_ref, window_ref, mixed_ref):
    row = pl.program_id(0)
    rows = pl.num_programs(0)
    kinds = taps_ref.shape[1]
    cols = local_ref.shape[1]
    parts = (far_west_ref, west_ref, local_ref, east_ref, far_east_ref)
    for index, part in enumerate(parts):
        window_ref[index * cols : (index + 1) * cols, :] = part[0]
    for kind in range(kinds):
        taps = taps_ref[0, kind : kind + 1, :]
        wide = jnp.broadcast_to(taps, (cols, taps.shape[1]))
        band = pltpu.roll(wide, 0, 1, stride=1, stride_axis=0).astype(jnp.bfloat16)
        response = jnp.dot(band, window_ref[...], preferred_element_type=jnp.float32)
        mixed_ref[kind, row] = jnp.dot(
            response.astype(jnp.bfloat16), weight_ref[kind], preferred_element_type=jnp.float32
        )

    @pl.when(row == rows - 1)
    def _():
        input_rows = mixed_ref.shape[1]
        output_rows = input_rows + 2 * RIM
        chunk = 16

        def body(step, carry):
            start = pl.multiple_of(step * chunk, chunk)
            edge_index = 0
            for out_row in range(output_rows):
                total = None
                for kind in range(kinds):
                    for in_row in range(max(0, out_row - 2 * RIM), min(input_rows, out_row + 1)):
                        scale = counts_ref[(out_row * kinds + kind) * input_rows + in_row]
                        term = scale * mixed_ref[kind, in_row, pl.ds(start, chunk), :]
                        total = term if total is None else total + term
                if RIM <= out_row < RIM + input_rows:
                    inner_ref[out_row - RIM, pl.ds(start, chunk), :] = total
                else:
                    edge_ref[edge_index, pl.ds(start, chunk), :] = total.astype(edge_ref.dtype)
                    edge_index += 1
            return carry

        lax.fori_loop(0, cols // chunk, body, 0)


def block_partials(counts, short_taps, parts, mix_weight):
    rows, cols, channels = parts[0].shape
    kinds = short_taps.shape[1]
    window = cols * len(parts)
    padded = jnp.pad(
        short_taps.astype(jnp.float32), ((0, 0), (0, 0), (0, window - short_taps.shape[2]))
    )
    part_spec = pl.BlockSpec((1, cols, channels), lambda i: (i, 0, 0))
    whole = lambda shape: pl.BlockSpec(shape, lambda i: (0,) * len(shape))
    return pl.pallas_call(
        _block_kernel,
        grid=(rows,),
        in_specs=[pl.BlockSpec(memory_space=pltpu.SMEM), pl.BlockSpec((1, kinds, window), lambda i: (i, 0, 0))]
        + [part_spec] * len(parts)
        + [whole(mix_weight.shape)],
        out_specs=[whole((2 * RIM, cols, channels)), whole((rows, cols, channels))],
        out_shape=[
            jax.ShapeDtypeStruct((2 * RIM, cols, channels), jnp.bfloat16),
            jax.ShapeDtypeStruct((rows, cols, channels), jnp.float32),
        ],
        scratch_shapes=[
            pltpu.VMEM((window, channels), jnp.bfloat16),
            pltpu.VMEM((kinds, rows, cols, mix_weight.shape[2]), jnp.float32),
        ],
        compiler_params=pltpu.CompilerParams(dimension_semantics=("arbitrary",)),
    )(counts.reshape(-1), padded, *parts, mix_weight)


def on_device(field, lon_width, lon_taps, row_scale, support, mix_weight):
    rows = field.shape[0]
    kinds = lon_taps.shape[1]
    far_west, west, east, far_east = longitude_halo(field)
    short_taps = masked_taps(lon_taps, lon_width)
    entries = support.shape[0]
    lists = with_halo(support, (("lat", 0),), entries)
    above = lists[:entries]
    below = lists[2 * entries :]
    out_rows = jnp.concatenate(
        [support[:, 0] + RIM, above[:, 0] - rows + RIM, below[:, 0] + rows + RIM]
    )
    in_rows = jnp.concatenate([support[:, 1], above[:, 1] - rows, below[:, 1] + rows])
    basis = jnp.concatenate([support[:, 2], above[:, 2], below[:, 2]])
    valid = jnp.concatenate(
        [(support[:, 1] >= 0) & (support[:, 1] < rows), above[:, 1] >= rows, below[:, 1] < 0]
    )
    counts = coupling(out_rows, in_rows, basis, valid, rows + 2 * RIM, rows, kinds)
    outgoing, inner = block_partials(
        counts, short_taps, (far_west, west, field, east, far_east), mix_weight
    )
    incoming = with_halo(outgoing, (("lat", 0),), RIM).astype(jnp.float32)
    inner = inner + jnp.pad(incoming[:RIM], ((0, rows - RIM), (0, 0), (0, 0)))
    inner = inner + jnp.pad(incoming[3 * RIM :], ((rows - RIM, 0), (0, 0), (0, 0)))
    return (inner * row_scale[:, None, None]).astype(jnp.bfloat16)


def solution(mesh):
    in_specs = (
        P("lat", "lon", None),
        P("lat"),
        P("lat", None, None),
        P("lat"),
        P("lat", None),
        P(),
    )
    out_specs = P("lat", "lon", None)
    return jax.shard_map(
        on_device, mesh=mesh, in_specs=in_specs, out_specs=out_specs, check_vma=False
    )
```

```python
import jax
import jax.numpy as jnp
from jax import lax
from jax.experimental import pallas as pl
from jax.experimental.pallas import tpu as pltpu
from jax.sharding import PartitionSpec as P

SPAN = 2
RIM = 2


def shifted(value, axis, by):
    length = lax.axis_size(axis)
    return lax.ppermute(value, axis, [(i, (i + by) % length) for i in range(length)])


def with_halo(block, sides, width):
    for axis, dim in sides:
        count = lax.axis_size(axis)
        forward = [(i, i + 1) for i in range(count - 1)]
        backward = [(target, source) for source, target in forward]
        low = lax.ppermute(
            lax.slice_in_dim(block, block.shape[dim] - width, None, axis=dim), axis, forward
        )
        high = lax.ppermute(lax.slice_in_dim(block, 0, width, axis=dim), axis, backward)
        block = jnp.concatenate([low, block, high], axis=dim)
    return block


def masked_taps(lon_taps, lon_width):
    length = lon_taps.shape[2]
    middle = (length - 1) // 2
    distance = jnp.abs(jnp.arange(length, dtype=jnp.int32) - middle)
    keep = distance[None, None, :] <= lon_width[:, None, None]
    return jnp.where(keep, lon_taps, 0.0).astype(jnp.bfloat16)


def longitude_halo(source):
    west = shifted(source, "lon", 1)
    east = shifted(source, "lon", -1)
    far_west = shifted(west, "lon", 1)
    far_east = shifted(east, "lon", -1)
    return far_west, west, east, far_east


def coupling(out_rows, in_rows, basis, valid, output_rows, input_rows, kinds):
    out_match = (out_rows[:, None] == jnp.arange(output_rows, dtype=jnp.int32)[None, :]) & valid[
        :, None
    ]
    in_match = (basis * input_rows + in_rows)[:, None] == jnp.arange(
        kinds * input_rows, dtype=jnp.int32
    )[None, :]
    table = jnp.dot(
        out_match.astype(jnp.float32).T,
        in_match.astype(jnp.float32),
        precision=lax.Precision.HIGHEST,
    )
    return table.reshape(output_rows, kinds, input_rows)


def _toeplitz_kernel(taps_ref, out_ref):
    kinds = taps_ref.shape[1]
    cols = out_ref.shape[2]
    for kind in range(kinds):
        row = taps_ref[0, kind : kind + 1, :]
        wide = jnp.broadcast_to(row, (cols, row.shape[1]))
        out_ref[0, kind] = pltpu.roll(wide, 0, 1, stride=1, stride_axis=0).astype(out_ref.dtype)


def band_matrix(short_taps, cols, window):
    rows, kinds, length = short_taps.shape
    padded = jnp.pad(short_taps.astype(jnp.float32), ((0, 0), (0, 0), (0, window - length)))
    return pl.pallas_call(
        _toeplitz_kernel,
        grid=(rows,),
        in_specs=[pl.BlockSpec((1, kinds, window), lambda i: (i, 0, 0))],
        out_specs=pl.BlockSpec((1, kinds, cols, window), lambda i: (i, 0, 0, 0)),
        out_shape=jax.ShapeDtypeStruct((rows, kinds, cols, window), jnp.bfloat16),
    )(padded)


def _block_kernel(counts_ref, band_ref, far_west_ref, west_ref, local_ref, east_ref, far_east_ref,
                  weight_ref, edge_ref, inner_ref, window_ref, response_ref, mixed_ref, total_ref):
    kind = pl.program_id(0)
    kinds = pl.num_programs(0)
    input_rows, cols, _ = local_ref.shape
    output_rows = input_rows + 2 * RIM
    parts = (far_west_ref, west_ref, local_ref, east_ref, far_east_ref)

    @pl.when(kind == 0)
    def _():
        for index, part in enumerate(parts):
            window_ref[:, index * cols : (index + 1) * cols, :] = part[...]
        total_ref[...] = jnp.zeros_like(total_ref)

    for in_row in range(input_rows):
        response = jnp.dot(band_ref[in_row, 0], window_ref[in_row], preferred_element_type=jnp.float32)
        response_ref[in_row * cols : (in_row + 1) * cols, :] = response.astype(jnp.bfloat16)
    mixed_ref[...] = jnp.dot(response_ref[...], weight_ref[0], preferred_element_type=jnp.float32)
    chunk = 16

    def body(step, carry):
        start = pl.multiple_of(step * chunk, chunk)
        pieces = [mixed_ref[pl.ds(in_row * cols + start, chunk), :] for in_row in range(input_rows)]
        for out_row in range(output_rows):
            total = total_ref[out_row, pl.ds(start, chunk), :]
            for in_row in range(max(0, out_row - 2 * RIM), min(input_rows, out_row + 1)):
                scale = counts_ref[(out_row * kinds + kind) * input_rows + in_row]
                total = total + scale * pieces[in_row]
            total_ref[out_row, pl.ds(start, chunk), :] = total
        return carry

    lax.fori_loop(0, cols // chunk, body, 0)

    @pl.when(kind == kinds - 1)
    def _():
        inner_ref[...] = total_ref[RIM : RIM + input_rows]
        edge_ref[:RIM] = total_ref[:RIM].astype(edge_ref.dtype)
        edge_ref[RIM:] = total_ref[RIM + input_rows :].astype(edge_ref.dtype)


def block_partials(counts, short_taps, parts, mix_weight):
    rows, cols, channels = parts[0].shape
    kinds = short_taps.shape[1]
    window = cols * len(parts)
    band = band_matrix(short_taps, cols, window)
    whole = lambda shape: pl.BlockSpec(shape, lambda k: (0,) * len(shape))
    return pl.pallas_call(
        _block_kernel,
        grid=(kinds,),
        in_specs=[
            pl.BlockSpec(memory_space=pltpu.SMEM),
            pl.BlockSpec((rows, 1, cols, window), lambda k: (0, k, 0, 0)),
        ]
        + [whole(parts[0].shape)] * len(parts)
        + [pl.BlockSpec((1,) + mix_weight.shape[1:], lambda k: (k, 0, 0))],
        out_specs=[whole((2 * RIM, cols, channels)), whole((rows, cols, channels))],
        out_shape=[
            jax.ShapeDtypeStruct((2 * RIM, cols, channels), jnp.bfloat16),
            jax.ShapeDtypeStruct((rows, cols, channels), jnp.float32),
        ],
        scratch_shapes=[
            pltpu.VMEM((rows, window, channels), jnp.bfloat16),
            pltpu.VMEM((rows * cols, channels), jnp.bfloat16),
            pltpu.VMEM((rows * cols, mix_weight.shape[2]), jnp.float32),
            pltpu.VMEM((rows + 2 * RIM, cols, mix_weight.shape[2]), jnp.float32),
        ],
        compiler_params=pltpu.CompilerParams(dimension_semantics=("arbitrary",)),
    )(counts.reshape(-1), band, *parts, mix_weight)


def on_device(field, lon_width, lon_taps, row_scale, support, mix_weight):
    rows = field.shape[0]
    kinds = lon_taps.shape[1]
    far_west, west, east, far_east = longitude_halo(field)
    short_taps = masked_taps(lon_taps, lon_width)
    entries = support.shape[0]
    lists = with_halo(support, (("lat", 0),), entries)
    above = lists[:entries]
    below = lists[2 * entries :]
    out_rows = jnp.concatenate(
        [support[:, 0] + RIM, above[:, 0] - rows + RIM, below[:, 0] + rows + RIM]
    )
    in_rows = jnp.concatenate([support[:, 1], above[:, 1] - rows, below[:, 1] + rows])
    basis = jnp.concatenate([support[:, 2], above[:, 2], below[:, 2]])
    valid = jnp.concatenate(
        [(support[:, 1] >= 0) & (support[:, 1] < rows), above[:, 1] >= rows, below[:, 1] < 0]
    )
    counts = coupling(out_rows, in_rows, basis, valid, rows + 2 * RIM, rows, kinds)
    outgoing, inner = block_partials(
        counts, short_taps, (far_west, west, field, east, far_east), mix_weight
    )
    incoming = with_halo(outgoing, (("lat", 0),), RIM).astype(jnp.float32)
    inner = inner + jnp.pad(incoming[:RIM], ((0, rows - RIM), (0, 0), (0, 0)))
    inner = inner + jnp.pad(incoming[3 * RIM :], ((rows - RIM, 0), (0, 0), (0, 0)))
    return (inner * row_scale[:, None, None]).astype(jnp.bfloat16)


def solution(mesh):
    in_specs = (
        P("lat", "lon", None),
        P("lat"),
        P("lat", None, None),
        P("lat"),
        P("lat", None),
        P(),
    )
    out_specs = P("lat", "lon", None)
    return jax.shard_map(
        on_device, mesh=mesh, in_specs=in_specs, out_specs=out_specs, check_vma=False
    )
```

```python
import functools

import jax
import jax.numpy as jnp
from jax import lax
from jax.experimental import pallas as pl
from jax.experimental.pallas import tpu as pltpu
from jax.sharding import PartitionSpec as P

SPAN = 2
RIM = 2


def shifted(value, axis, by):
    length = lax.axis_size(axis)
    return lax.ppermute(value, axis, [(i, (i + by) % length) for i in range(length)])


def with_halo(block, sides, width):
    for axis, dim in sides:
        count = lax.axis_size(axis)
        forward = [(i, i + 1) for i in range(count - 1)]
        backward = [(target, source) for source, target in forward]
        low = lax.ppermute(
            lax.slice_in_dim(block, block.shape[dim] - width, None, axis=dim), axis, forward
        )
        high = lax.ppermute(lax.slice_in_dim(block, 0, width, axis=dim), axis, backward)
        block = jnp.concatenate([low, block, high], axis=dim)
    return block


def masked_taps(lon_taps, lon_width):
    length = lon_taps.shape[2]
    middle = (length - 1) // 2
    distance = jnp.abs(jnp.arange(length, dtype=jnp.int32) - middle)
    keep = distance[None, None, :] <= lon_width[:, None, None]
    return jnp.where(keep, lon_taps, 0.0).astype(jnp.bfloat16)


def longitude_halo(source):
    west = shifted(source, "lon", 1)
    east = shifted(source, "lon", -1)
    far_west = shifted(west, "lon", 1)
    far_east = shifted(east, "lon", -1)
    return far_west, west, east, far_east


def coupling(out_rows, in_rows, basis, valid, output_rows, input_rows, kinds):
    out_match = (out_rows[:, None] == jnp.arange(output_rows, dtype=jnp.int32)[None, :]) & valid[
        :, None
    ]
    in_match = (basis * input_rows + in_rows)[:, None] == jnp.arange(
        kinds * input_rows, dtype=jnp.int32
    )[None, :]
    table = jnp.dot(
        out_match.astype(jnp.float32).T,
        in_match.astype(jnp.float32),
        precision=lax.Precision.HIGHEST,
    )
    return table.reshape(output_rows, kinds, input_rows)


def _toeplitz_kernel(taps_ref, out_ref):
    kinds = taps_ref.shape[1]
    cols = out_ref.shape[2]
    for kind in range(kinds):
        row = taps_ref[0, kind : kind + 1, :]
        wide = jnp.broadcast_to(row, (cols, row.shape[1]))
        out_ref[0, kind] = pltpu.roll(wide, 0, 1, stride=1, stride_axis=0).astype(out_ref.dtype)


def band_matrix(short_taps, cols, window):
    rows, kinds, length = short_taps.shape
    padded = jnp.pad(short_taps.astype(jnp.float32), ((0, 0), (0, 0), (0, window - length)))
    return pl.pallas_call(
        _toeplitz_kernel,
        grid=(rows,),
        in_specs=[pl.BlockSpec((1, kinds, window), lambda i: (i, 0, 0))],
        out_specs=pl.BlockSpec((1, kinds, cols, window), lambda i: (i, 0, 0, 0)),
        out_shape=jax.ShapeDtypeStruct((rows, kinds, cols, window), jnp.bfloat16),
    )(padded)


def _block_kernel(first, counts_ref, band_ref, far_west_ref, west_ref, local_ref, east_ref,
                  far_east_ref, weight_ref, total_ref, window_ref, response_ref, mixed_ref):
    kind = pl.program_id(0)
    kinds = pl.num_programs(0)
    group, cols, _ = local_ref.shape
    reach = group + 2 * RIM
    parts = (far_west_ref, west_ref, local_ref, east_ref, far_east_ref)

    @pl.when(kind == 0)
    def _():
        for index, part in enumerate(parts):
            window_ref[:, index * cols : (index + 1) * cols, :] = part[...]
        total_ref[...] = jnp.zeros_like(total_ref)

    for in_row in range(group):
        response = jnp.dot(band_ref[in_row, 0], window_ref[in_row], preferred_element_type=jnp.float32)
        response_ref[in_row * cols : (in_row + 1) * cols, :] = response.astype(jnp.bfloat16)
    mixed_ref[...] = jnp.dot(response_ref[...], weight_ref[0], preferred_element_type=jnp.float32)
    chunk = 16
    rows = first[1]

    def body(step, carry):
        start = pl.multiple_of(step * chunk, chunk)
        pieces = [mixed_ref[pl.ds(in_row * cols + start, chunk), :] for in_row in range(group)]
        for out_row in range(reach):
            total = total_ref[out_row, pl.ds(start, chunk), :]
            for in_row in range(max(0, out_row - 2 * RIM), min(group, out_row + 1)):
                where = ((first[0] + out_row) * kinds + kind) * rows + first[0] + in_row
                total = total + counts_ref[where] * pieces[in_row]
            total_ref[out_row, pl.ds(start, chunk), :] = total
        return carry

    lax.fori_loop(0, cols // chunk, body, 0)


def block_partials(counts, band, parts, mix_weight, first, group):
    rows, cols, channels = parts[2].shape
    kinds = band.shape[1]
    window = band.shape[3]
    index = first // group

    def rows_of(part):
        if part.shape[0] == group:
            return pl.BlockSpec((group, cols, channels), lambda k: (0, 0, 0))
        return pl.BlockSpec((group, cols, channels), lambda k: (index, 0, 0))

    kernel = functools.partial(_block_kernel, (first, rows))
    return pl.pallas_call(
        kernel,
        grid=(kinds,),
        in_specs=[
            pl.BlockSpec(memory_space=pltpu.SMEM),
            pl.BlockSpec((group, 1, cols, window), lambda k: (index, k, 0, 0)),
        ]
        + [rows_of(part) for part in parts]
        + [pl.BlockSpec((1,) + mix_weight.shape[1:], lambda k: (k, 0, 0))],
        out_specs=pl.BlockSpec((group + 2 * RIM, cols, channels), lambda k: (0, 0, 0)),
        out_shape=jax.ShapeDtypeStruct((group + 2 * RIM, cols, channels), jnp.float32),
        scratch_shapes=[
            pltpu.VMEM((group, window, channels), jnp.bfloat16),
            pltpu.VMEM((group * cols, channels), jnp.bfloat16),
            pltpu.VMEM((group * cols, mix_weight.shape[2]), jnp.float32),
        ],
        compiler_params=pltpu.CompilerParams(dimension_semantics=("arbitrary",)),
    )(counts.reshape(-1), band, *parts, mix_weight)


def on_device(field, lon_width, lon_taps, row_scale, support, mix_weight):
    rows, cols, _ = field.shape
    kinds = lon_taps.shape[1]
    group = rows // 2
    west = shifted(field, "lon", 1)
    east = shifted(field, "lon", -1)
    short_taps = masked_taps(lon_taps, lon_width)
    band = band_matrix(short_taps, cols, cols * (2 * SPAN + 1))
    entries = support.shape[0]
    lists = with_halo(support, (("lat", 0),), entries)
    above = lists[:entries]
    below = lists[2 * entries :]
    out_rows = jnp.concatenate(
        [support[:, 0] + RIM, above[:, 0] - rows + RIM, below[:, 0] + rows + RIM]
    )
    in_rows = jnp.concatenate([support[:, 1], above[:, 1] - rows, below[:, 1] + rows])
    basis = jnp.concatenate([support[:, 2], above[:, 2], below[:, 2]])
    valid = jnp.concatenate(
        [(support[:, 1] >= 0) & (support[:, 1] < rows), above[:, 1] >= rows, below[:, 1] < 0]
    )
    counts = coupling(out_rows, in_rows, basis, valid, rows + 2 * RIM, rows, kinds)
    count = lax.axis_size("lat")
    forward = [(i, i + 1) for i in range(count - 1)]
    backward = [(target, source) for source, target in forward]
    far_west = shifted(west[:group], "lon", 1)
    far_east = shifted(east[:group], "lon", -1)
    far_west, far_east, next_west, next_east = lax.optimization_barrier(
        (far_west, far_east, west[group:], east[group:])
    )
    later_west = shifted(next_west, "lon", 1)
    later_east = shifted(next_east, "lon", -1)
    parts = (far_west, west, field, east, far_east)
    upper = block_partials(counts, band, parts, mix_weight, 0, group)
    from_below = lax.ppermute(upper[:RIM].astype(jnp.bfloat16), "lat", backward)
    from_below, later_west, later_east = lax.optimization_barrier(
        (from_below, later_west, later_east)
    )
    parts = (later_west, west, field, east, later_east)
    lower = block_partials(counts, band, parts, mix_weight, group, group)
    from_above = lax.ppermute(lower[group + RIM :].astype(jnp.bfloat16), "lat", forward)
    inner = upper[RIM:] + lower[: group + RIM]
    inner = inner + jnp.pad(from_above.astype(jnp.float32), ((0, rows - RIM), (0, 0), (0, 0)))
    inner = inner + jnp.pad(from_below.astype(jnp.float32), ((rows - RIM, 0), (0, 0), (0, 0)))
    return (inner * row_scale[:, None, None]).astype(jnp.bfloat16)


def solution(mesh):
    in_specs = (
        P("lat", "lon", None),
        P("lat"),
        P("lat", None, None),
        P("lat"),
        P("lat", None),
        P(),
    )
    out_specs = P("lat", "lon", None)
    return jax.shard_map(
        on_device, mesh=mesh, in_specs=in_specs, out_specs=out_specs, check_vma=False
    )
```

```python
import jax
import jax.numpy as jnp
from jax import lax
from jax.experimental import pallas as pl
from jax.experimental.pallas import tpu as pltpu
from jax.sharding import PartitionSpec as P

SPAN = 2
RIM = 2


def shifted(value, axis, by):
    length = lax.axis_size(axis)
    return lax.ppermute(value, axis, [(i, (i + by) % length) for i in range(length)])


def with_halo(block, sides, width):
    for axis, dim in sides:
        count = lax.axis_size(axis)
        forward = [(i, i + 1) for i in range(count - 1)]
        backward = [(target, source) for source, target in forward]
        low = lax.ppermute(
            lax.slice_in_dim(block, block.shape[dim] - width, None, axis=dim), axis, forward
        )
        high = lax.ppermute(lax.slice_in_dim(block, 0, width, axis=dim), axis, backward)
        block = jnp.concatenate([low, block, high], axis=dim)
    return block


def masked_taps(lon_taps, lon_width):
    length = lon_taps.shape[2]
    middle = (length - 1) // 2
    distance = jnp.abs(jnp.arange(length, dtype=jnp.int32) - middle)
    keep = distance[None, None, :] <= lon_width[:, None, None]
    return jnp.where(keep, lon_taps, 0.0).astype(jnp.bfloat16)


def crossed(value, by):
    bands = lax.axis_size("lat")
    length = lax.axis_size("lon")
    pairs = []
    for band in range(bands):
        step = by if band % 2 == 0 else -by
        for cell in range(length):
            pairs.append((band * length + cell, band * length + (cell + step) % length))
    return lax.ppermute(value, ("lat", "lon"), pairs)


def longitude_halo(source):
    near_one = crossed(source, 1)
    near_two = crossed(source, -1)
    far_one = crossed(near_one, 1)
    far_two = crossed(near_two, -1)
    return far_one, near_one, near_two, far_two


def coupling(out_rows, in_rows, basis, valid, output_rows, input_rows, kinds):
    out_match = (out_rows[:, None] == jnp.arange(output_rows, dtype=jnp.int32)[None, :]) & valid[
        :, None
    ]
    in_match = (basis * input_rows + in_rows)[:, None] == jnp.arange(
        kinds * input_rows, dtype=jnp.int32
    )[None, :]
    table = jnp.dot(
        out_match.astype(jnp.float32).T,
        in_match.astype(jnp.float32),
        precision=lax.Precision.HIGHEST,
    )
    return table.reshape(output_rows, kinds, input_rows)


def _toeplitz_kernel(taps_ref, out_ref):
    kinds = taps_ref.shape[1]
    cols = out_ref.shape[2]
    for kind in range(kinds):
        row = taps_ref[0, kind : kind + 1, :]
        wide = jnp.broadcast_to(row, (cols, row.shape[1]))
        out_ref[0, kind] = pltpu.roll(wide, 0, 1, stride=1, stride_axis=0).astype(out_ref.dtype)


def band_matrix(short_taps, cols, window):
    rows, kinds, length = short_taps.shape
    padded = jnp.pad(short_taps.astype(jnp.float32), ((0, 0), (0, 0), (0, window - length)))
    return pl.pallas_call(
        _toeplitz_kernel,
        grid=(rows,),
        in_specs=[pl.BlockSpec((1, kinds, window), lambda i: (i, 0, 0))],
        out_specs=pl.BlockSpec((1, kinds, cols, window), lambda i: (i, 0, 0, 0)),
        out_shape=jax.ShapeDtypeStruct((rows, kinds, cols, window), jnp.bfloat16),
    )(padded)


def _block_kernel(parity_ref, counts_ref, band_ref, far_west_ref, west_ref, local_ref, east_ref, far_east_ref,
                  weight_ref, edge_ref, inner_ref, window_ref, response_ref, mixed_ref, total_ref):
    kind = pl.program_id(0)
    kinds = pl.num_programs(0)
    input_rows, cols, _ = local_ref.shape
    output_rows = input_rows + 2 * RIM
    parts = (far_west_ref, west_ref, local_ref, east_ref, far_east_ref)

    @pl.when((kind == 0) & (parity_ref[0] == 0))
    def _():
        for index, part in enumerate(parts):
            window_ref[:, index * cols : (index + 1) * cols, :] = part[...]

    @pl.when((kind == 0) & (parity_ref[0] != 0))
    def _():
        for index, part in enumerate(parts[::-1]):
            window_ref[:, index * cols : (index + 1) * cols, :] = part[...]

    @pl.when(kind == 0)
    def _():
        total_ref[...] = jnp.zeros_like(total_ref)

    for in_row in range(input_rows):
        response = jnp.dot(band_ref[in_row, 0], window_ref[in_row], preferred_element_type=jnp.float32)
        response_ref[in_row * cols : (in_row + 1) * cols, :] = response.astype(jnp.bfloat16)
    mixed_ref[...] = jnp.dot(response_ref[...], weight_ref[0], preferred_element_type=jnp.float32)
    chunk = 16

    def body(step, carry):
        start = pl.multiple_of(step * chunk, chunk)
        pieces = [mixed_ref[pl.ds(in_row * cols + start, chunk), :] for in_row in range(input_rows)]
        for out_row in range(output_rows):
            total = total_ref[out_row, pl.ds(start, chunk), :]
            for in_row in range(max(0, out_row - 2 * RIM), min(input_rows, out_row + 1)):
                scale = counts_ref[(out_row * kinds + kind) * input_rows + in_row]
                total = total + scale * pieces[in_row]
            total_ref[out_row, pl.ds(start, chunk), :] = total
        return carry

    lax.fori_loop(0, cols // chunk, body, 0)

    @pl.when(kind == kinds - 1)
    def _():
        inner_ref[...] = total_ref[RIM : RIM + input_rows]
        edge_ref[:RIM] = total_ref[:RIM].astype(edge_ref.dtype)
        edge_ref[RIM:] = total_ref[RIM + input_rows :].astype(edge_ref.dtype)


def block_partials(parity, counts, short_taps, parts, mix_weight):
    rows, cols, channels = parts[0].shape
    kinds = short_taps.shape[1]
    window = cols * len(parts)
    band = band_matrix(short_taps, cols, window)
    whole = lambda shape: pl.BlockSpec(shape, lambda k: (0,) * len(shape))
    return pl.pallas_call(
        _block_kernel,
        grid=(kinds,),
        in_specs=[
            pl.BlockSpec(memory_space=pltpu.SMEM),
            pl.BlockSpec(memory_space=pltpu.SMEM),
            pl.BlockSpec((rows, 1, cols, window), lambda k: (0, k, 0, 0)),
        ]
        + [whole(parts[0].shape)] * len(parts)
        + [pl.BlockSpec((1,) + mix_weight.shape[1:], lambda k: (k, 0, 0))],
        out_specs=[whole((2 * RIM, cols, channels)), whole((rows, cols, channels))],
        out_shape=[
            jax.ShapeDtypeStruct((2 * RIM, cols, channels), jnp.bfloat16),
            jax.ShapeDtypeStruct((rows, cols, channels), jnp.float32),
        ],
        scratch_shapes=[
            pltpu.VMEM((rows, window, channels), jnp.bfloat16),
            pltpu.VMEM((rows * cols, channels), jnp.bfloat16),
            pltpu.VMEM((rows * cols, mix_weight.shape[2]), jnp.float32),
            pltpu.VMEM((rows + 2 * RIM, cols, mix_weight.shape[2]), jnp.float32),
        ],
        compiler_params=pltpu.CompilerParams(dimension_semantics=("arbitrary",)),
    )(parity, counts.reshape(-1), band, *parts, mix_weight)


def on_device(field, lon_width, lon_taps, row_scale, support, mix_weight):
    rows = field.shape[0]
    kinds = lon_taps.shape[1]
    far_west, west, east, far_east = longitude_halo(field)
    short_taps = masked_taps(lon_taps, lon_width)
    entries = support.shape[0]
    lists = with_halo(support, (("lat", 0),), entries)
    above = lists[:entries]
    below = lists[2 * entries :]
    out_rows = jnp.concatenate(
        [support[:, 0] + RIM, above[:, 0] - rows + RIM, below[:, 0] + rows + RIM]
    )
    in_rows = jnp.concatenate([support[:, 1], above[:, 1] - rows, below[:, 1] + rows])
    basis = jnp.concatenate([support[:, 2], above[:, 2], below[:, 2]])
    valid = jnp.concatenate(
        [(support[:, 1] >= 0) & (support[:, 1] < rows), above[:, 1] >= rows, below[:, 1] < 0]
    )
    counts = coupling(out_rows, in_rows, basis, valid, rows + 2 * RIM, rows, kinds)
    parity = (lax.axis_index("lat") % 2).astype(jnp.int32).reshape(1)
    outgoing, inner = block_partials(
        parity, counts, short_taps, (far_west, west, field, east, far_east), mix_weight
    )
    incoming = with_halo(outgoing, (("lat", 0),), RIM).astype(jnp.float32)
    inner = inner + jnp.pad(incoming[:RIM], ((0, rows - RIM), (0, 0), (0, 0)))
    inner = inner + jnp.pad(incoming[3 * RIM :], ((rows - RIM, 0), (0, 0), (0, 0)))
    return (inner * row_scale[:, None, None]).astype(jnp.bfloat16)


def solution(mesh):
    in_specs = (
        P("lat", "lon", None),
        P("lat"),
        P("lat", None, None),
        P("lat"),
        P("lat", None),
        P(),
    )
    out_specs = P("lat", "lon", None)
    return jax.shard_map(
        on_device, mesh=mesh, in_specs=in_specs, out_specs=out_specs, check_vma=False
    )
```

```python
import jax
import jax.numpy as jnp
from jax import lax
from jax.experimental import pallas as pl
from jax.experimental.pallas import tpu as pltpu
from jax.sharding import PartitionSpec as P

SPAN = 2
RIM = 2


def shifted(value, axis, by):
    length = lax.axis_size(axis)
    return lax.ppermute(value, axis, [(i, (i + by) % length) for i in range(length)])


def with_halo(block, sides, width):
    for axis, dim in sides:
        count = lax.axis_size(axis)
        forward = [(i, i + 1) for i in range(count - 1)]
        backward = [(target, source) for source, target in forward]
        low = lax.ppermute(
            lax.slice_in_dim(block, block.shape[dim] - width, None, axis=dim), axis, forward
        )
        high = lax.ppermute(lax.slice_in_dim(block, 0, width, axis=dim), axis, backward)
        block = jnp.concatenate([low, block, high], axis=dim)
    return block


def masked_taps(lon_taps, lon_width):
    length = lon_taps.shape[2]
    middle = (length - 1) // 2
    distance = jnp.abs(jnp.arange(length, dtype=jnp.int32) - middle)
    keep = distance[None, None, :] <= lon_width[:, None, None]
    return jnp.where(keep, lon_taps, 0.0).astype(jnp.bfloat16)


def longitude_halo(source, support):
    west = shifted(source, "lon", 1)
    east = shifted(source, "lon", -1)
    west, east, support = lax.optimization_barrier((west, east, support))
    far_west = shifted(west, "lon", 1)
    far_east = shifted(east, "lon", -1)
    return far_west, west, east, far_east, support


def coupling(out_rows, in_rows, basis, valid, output_rows, input_rows, kinds):
    out_match = (out_rows[:, None] == jnp.arange(output_rows, dtype=jnp.int32)[None, :]) & valid[
        :, None
    ]
    in_match = (basis * input_rows + in_rows)[:, None] == jnp.arange(
        kinds * input_rows, dtype=jnp.int32
    )[None, :]
    table = jnp.dot(
        out_match.astype(jnp.float32).T,
        in_match.astype(jnp.float32),
        precision=lax.Precision.HIGHEST,
    )
    return table.reshape(output_rows, kinds, input_rows)


def _toeplitz_kernel(taps_ref, out_ref):
    kinds = taps_ref.shape[1]
    cols = out_ref.shape[2]
    for kind in range(kinds):
        row = taps_ref[0, kind : kind + 1, :]
        wide = jnp.broadcast_to(row, (cols, row.shape[1]))
        out_ref[0, kind] = pltpu.roll(wide, 0, 1, stride=1, stride_axis=0).astype(out_ref.dtype)


def band_matrix(short_taps, cols, window):
    rows, kinds, length = short_taps.shape
    padded = jnp.pad(short_taps.astype(jnp.float32), ((0, 0), (0, 0), (0, window - length)))
    return pl.pallas_call(
        _toeplitz_kernel,
        grid=(rows,),
        in_specs=[pl.BlockSpec((1, kinds, window), lambda i: (i, 0, 0))],
        out_specs=pl.BlockSpec((1, kinds, cols, window), lambda i: (i, 0, 0, 0)),
        out_shape=jax.ShapeDtypeStruct((rows, kinds, cols, window), jnp.bfloat16),
    )(padded)


def _block_kernel(counts_ref, band_ref, far_west_ref, west_ref, local_ref, east_ref, far_east_ref,
                  weight_ref, edge_ref, inner_ref, window_ref, response_ref, mixed_ref, total_ref):
    kind = pl.program_id(0)
    kinds = pl.num_programs(0)
    input_rows, cols, _ = local_ref.shape
    output_rows = input_rows + 2 * RIM
    parts = (far_west_ref, west_ref, local_ref, east_ref, far_east_ref)

    @pl.when(kind == 0)
    def _():
        for index, part in enumerate(parts):
            window_ref[:, index * cols : (index + 1) * cols, :] = part[...]
        total_ref[...] = jnp.zeros_like(total_ref)

    for in_row in range(input_rows):
        response = jnp.dot(band_ref[in_row, 0], window_ref[in_row], preferred_element_type=jnp.float32)
        response_ref[in_row * cols : (in_row + 1) * cols, :] = response.astype(jnp.bfloat16)
    mixed_ref[...] = jnp.dot(response_ref[...], weight_ref[0], preferred_element_type=jnp.float32)
    chunk = 16

    def body(step, carry):
        start = pl.multiple_of(step * chunk, chunk)
        pieces = [mixed_ref[pl.ds(in_row * cols + start, chunk), :] for in_row in range(input_rows)]
        for out_row in range(output_rows):
            total = total_ref[out_row, pl.ds(start, chunk), :]
            for in_row in range(max(0, out_row - 2 * RIM), min(input_rows, out_row + 1)):
                scale = counts_ref[(out_row * kinds + kind) * input_rows + in_row]
                total = total + scale * pieces[in_row]
            total_ref[out_row, pl.ds(start, chunk), :] = total
        return carry

    lax.fori_loop(0, cols // chunk, body, 0)

    @pl.when(kind == kinds - 1)
    def _():
        inner_ref[...] = total_ref[RIM : RIM + input_rows]
        edge_ref[:RIM] = total_ref[:RIM].astype(edge_ref.dtype)
        edge_ref[RIM:] = total_ref[RIM + input_rows :].astype(edge_ref.dtype)


def block_partials(counts, short_taps, parts, mix_weight):
    rows, cols, channels = parts[0].shape
    kinds = short_taps.shape[1]
    window = cols * len(parts)
    band = band_matrix(short_taps, cols, window)
    whole = lambda shape: pl.BlockSpec(shape, lambda k: (0,) * len(shape))
    return pl.pallas_call(
        _block_kernel,
        grid=(kinds,),
        in_specs=[
            pl.BlockSpec(memory_space=pltpu.SMEM),
            pl.BlockSpec((rows, 1, cols, window), lambda k: (0, k, 0, 0)),
        ]
        + [whole(parts[0].shape)] * len(parts)
        + [pl.BlockSpec((1,) + mix_weight.shape[1:], lambda k: (k, 0, 0))],
        out_specs=[whole((2 * RIM, cols, channels)), whole((rows, cols, channels))],
        out_shape=[
            jax.ShapeDtypeStruct((2 * RIM, cols, channels), jnp.bfloat16),
            jax.ShapeDtypeStruct((rows, cols, channels), jnp.float32),
        ],
        scratch_shapes=[
            pltpu.VMEM((rows, window, channels), jnp.bfloat16),
            pltpu.VMEM((rows * cols, channels), jnp.bfloat16),
            pltpu.VMEM((rows * cols, mix_weight.shape[2]), jnp.float32),
            pltpu.VMEM((rows + 2 * RIM, cols, mix_weight.shape[2]), jnp.float32),
        ],
        compiler_params=pltpu.CompilerParams(dimension_semantics=("arbitrary",)),
    )(counts.reshape(-1), band, *parts, mix_weight)


def on_device(field, lon_width, lon_taps, row_scale, support, mix_weight):
    rows = field.shape[0]
    kinds = lon_taps.shape[1]
    far_west, west, east, far_east, support = longitude_halo(field, support)
    short_taps = masked_taps(lon_taps, lon_width)
    entries = support.shape[0]
    lists = with_halo(support, (("lat", 0),), entries)
    above = lists[:entries]
    below = lists[2 * entries :]
    out_rows = jnp.concatenate(
        [support[:, 0] + RIM, above[:, 0] - rows + RIM, below[:, 0] + rows + RIM]
    )
    in_rows = jnp.concatenate([support[:, 1], above[:, 1] - rows, below[:, 1] + rows])
    basis = jnp.concatenate([support[:, 2], above[:, 2], below[:, 2]])
    valid = jnp.concatenate(
        [(support[:, 1] >= 0) & (support[:, 1] < rows), above[:, 1] >= rows, below[:, 1] < 0]
    )
    counts = coupling(out_rows, in_rows, basis, valid, rows + 2 * RIM, rows, kinds)
    outgoing, inner = block_partials(
        counts, short_taps, (far_west, west, field, east, far_east), mix_weight
    )
    incoming = with_halo(outgoing, (("lat", 0),), RIM).astype(jnp.float32)
    inner = inner + jnp.pad(incoming[:RIM], ((0, rows - RIM), (0, 0), (0, 0)))
    inner = inner + jnp.pad(incoming[3 * RIM :], ((rows - RIM, 0), (0, 0), (0, 0)))
    return (inner * row_scale[:, None, None]).astype(jnp.bfloat16)


def solution(mesh):
    in_specs = (
        P("lat", "lon", None),
        P("lat"),
        P("lat", None, None),
        P("lat"),
        P("lat", None),
        P(),
    )
    out_specs = P("lat", "lon", None)
    return jax.shard_map(
        on_device, mesh=mesh, in_specs=in_specs, out_specs=out_specs, check_vma=False
    )
```

```python
import jax
import jax.numpy as jnp
from jax import lax
from jax.experimental import pallas as pl
from jax.experimental.pallas import tpu as pltpu
from jax.sharding import PartitionSpec as P

SPAN = 2
RIM = 2


def shifted(value, axis, by):
    length = lax.axis_size(axis)
    return lax.ppermute(value, axis, [(i, (i + by) % length) for i in range(length)])


def with_halo(block, sides, width):
    for axis, dim in sides:
        count = lax.axis_size(axis)
        forward = [(i, i + 1) for i in range(count - 1)]
        backward = [(target, source) for source, target in forward]
        low = lax.ppermute(
            lax.slice_in_dim(block, block.shape[dim] - width, None, axis=dim), axis, forward
        )
        high = lax.ppermute(lax.slice_in_dim(block, 0, width, axis=dim), axis, backward)
        block = jnp.concatenate([low, block, high], axis=dim)
    return block


def masked_taps(lon_taps, lon_width):
    length = lon_taps.shape[2]
    middle = (length - 1) // 2
    distance = jnp.abs(jnp.arange(length, dtype=jnp.int32) - middle)
    keep = distance[None, None, :] <= lon_width[:, None, None]
    return jnp.where(keep, lon_taps, 0.0).astype(jnp.bfloat16)


def longitude_halo(source, support):
    west = shifted(source, "lon", 1)
    east = shifted(source, "lon", -1)
    far_west = shifted(west, "lon", 1)
    far_east = shifted(east, "lon", -1)
    far_west, far_east, support = lax.optimization_barrier((far_west, far_east, support))
    return far_west, west, east, far_east, support


def coupling(out_rows, in_rows, basis, valid, output_rows, input_rows, kinds):
    out_match = (out_rows[:, None] == jnp.arange(output_rows, dtype=jnp.int32)[None, :]) & valid[
        :, None
    ]
    in_match = (basis * input_rows + in_rows)[:, None] == jnp.arange(
        kinds * input_rows, dtype=jnp.int32
    )[None, :]
    table = jnp.dot(
        out_match.astype(jnp.float32).T,
        in_match.astype(jnp.float32),
        precision=lax.Precision.HIGHEST,
    )
    return table.reshape(output_rows, kinds, input_rows)


def _toeplitz_kernel(taps_ref, out_ref):
    kinds = taps_ref.shape[1]
    cols = out_ref.shape[2]
    for kind in range(kinds):
        row = taps_ref[0, kind : kind + 1, :]
        wide = jnp.broadcast_to(row, (cols, row.shape[1]))
        out_ref[0, kind] = pltpu.roll(wide, 0, 1, stride=1, stride_axis=0).astype(out_ref.dtype)


def band_matrix(short_taps, cols, window):
    rows, kinds, length = short_taps.shape
    padded = jnp.pad(short_taps.astype(jnp.float32), ((0, 0), (0, 0), (0, window - length)))
    return pl.pallas_call(
        _toeplitz_kernel,
        grid=(rows,),
        in_specs=[pl.BlockSpec((1, kinds, window), lambda i: (i, 0, 0))],
        out_specs=pl.BlockSpec((1, kinds, cols, window), lambda i: (i, 0, 0, 0)),
        out_shape=jax.ShapeDtypeStruct((rows, kinds, cols, window), jnp.bfloat16),
    )(padded)


def _block_kernel(counts_ref, band_ref, far_west_ref, west_ref, local_ref, east_ref, far_east_ref,
                  weight_ref, edge_ref, inner_ref, window_ref, response_ref, mixed_ref, total_ref):
    kind = pl.program_id(0)
    kinds = pl.num_programs(0)
    input_rows, cols, _ = local_ref.shape
    output_rows = input_rows + 2 * RIM
    parts = (far_west_ref, west_ref, local_ref, east_ref, far_east_ref)

    @pl.when(kind == 0)
    def _():
        for index, part in enumerate(parts):
            window_ref[:, index * cols : (index + 1) * cols, :] = part[...]
        total_ref[...] = jnp.zeros_like(total_ref)

    for in_row in range(input_rows):
        response = jnp.dot(band_ref[in_row, 0], window_ref[in_row], preferred_element_type=jnp.float32)
        response_ref[in_row * cols : (in_row + 1) * cols, :] = response.astype(jnp.bfloat16)
    mixed_ref[...] = jnp.dot(response_ref[...], weight_ref[0], preferred_element_type=jnp.float32)
    chunk = 16

    def body(step, carry):
        start = pl.multiple_of(step * chunk, chunk)
        pieces = [mixed_ref[pl.ds(in_row * cols + start, chunk), :] for in_row in range(input_rows)]
        for out_row in range(output_rows):
            total = total_ref[out_row, pl.ds(start, chunk), :]
            for in_row in range(max(0, out_row - 2 * RIM), min(input_rows, out_row + 1)):
                scale = counts_ref[(out_row * kinds + kind) * input_rows + in_row]
                total = total + scale * pieces[in_row]
            total_ref[out_row, pl.ds(start, chunk), :] = total
        return carry

    lax.fori_loop(0, cols // chunk, body, 0)

    @pl.when(kind == kinds - 1)
    def _():
        inner_ref[...] = total_ref[RIM : RIM + input_rows]
        edge_ref[:RIM] = total_ref[:RIM].astype(edge_ref.dtype)
        edge_ref[RIM:] = total_ref[RIM + input_rows :].astype(edge_ref.dtype)


def block_partials(counts, short_taps, parts, mix_weight):
    rows, cols, channels = parts[0].shape
    kinds = short_taps.shape[1]
    window = cols * len(parts)
    band = band_matrix(short_taps, cols, window)
    whole = lambda shape: pl.BlockSpec(shape, lambda k: (0,) * len(shape))
    return pl.pallas_call(
        _block_kernel,
        grid=(kinds,),
        in_specs=[
            pl.BlockSpec(memory_space=pltpu.SMEM),
            pl.BlockSpec((rows, 1, cols, window), lambda k: (0, k, 0, 0)),
        ]
        + [whole(parts[0].shape)] * len(parts)
        + [pl.BlockSpec((1,) + mix_weight.shape[1:], lambda k: (k, 0, 0))],
        out_specs=[whole((2 * RIM, cols, channels)), whole((rows, cols, channels))],
        out_shape=[
            jax.ShapeDtypeStruct((2 * RIM, cols, channels), jnp.bfloat16),
            jax.ShapeDtypeStruct((rows, cols, channels), jnp.float32),
        ],
        scratch_shapes=[
            pltpu.VMEM((rows, window, channels), jnp.bfloat16),
            pltpu.VMEM((rows * cols, channels), jnp.bfloat16),
            pltpu.VMEM((rows * cols, mix_weight.shape[2]), jnp.float32),
            pltpu.VMEM((rows + 2 * RIM, cols, mix_weight.shape[2]), jnp.float32),
        ],
        compiler_params=pltpu.CompilerParams(dimension_semantics=("arbitrary",)),
    )(counts.reshape(-1), band, *parts, mix_weight)


def on_device(field, lon_width, lon_taps, row_scale, support, mix_weight):
    rows = field.shape[0]
    kinds = lon_taps.shape[1]
    far_west, west, east, far_east, support = longitude_halo(field, support)
    short_taps = masked_taps(lon_taps, lon_width)
    entries = support.shape[0]
    lists = with_halo(support, (("lat", 0),), entries)
    above = lists[:entries]
    below = lists[2 * entries :]
    out_rows = jnp.concatenate(
        [support[:, 0] + RIM, above[:, 0] - rows + RIM, below[:, 0] + rows + RIM]
    )
    in_rows = jnp.concatenate([support[:, 1], above[:, 1] - rows, below[:, 1] + rows])
    basis = jnp.concatenate([support[:, 2], above[:, 2], below[:, 2]])
    valid = jnp.concatenate(
        [(support[:, 1] >= 0) & (support[:, 1] < rows), above[:, 1] >= rows, below[:, 1] < 0]
    )
    counts = coupling(out_rows, in_rows, basis, valid, rows + 2 * RIM, rows, kinds)
    outgoing, inner = block_partials(
        counts, short_taps, (far_west, west, field, east, far_east), mix_weight
    )
    incoming = with_halo(outgoing, (("lat", 0),), RIM).astype(jnp.float32)
    inner = inner + jnp.pad(incoming[:RIM], ((0, rows - RIM), (0, 0), (0, 0)))
    inner = inner + jnp.pad(incoming[3 * RIM :], ((rows - RIM, 0), (0, 0), (0, 0)))
    return (inner * row_scale[:, None, None]).astype(jnp.bfloat16)


def solution(mesh):
    in_specs = (
        P("lat", "lon", None),
        P("lat"),
        P("lat", None, None),
        P("lat"),
        P("lat", None),
        P(),
    )
    out_specs = P("lat", "lon", None)
    return jax.shard_map(
        on_device, mesh=mesh, in_specs=in_specs, out_specs=out_specs, check_vma=False
    )
```

```python
import jax
import jax.numpy as jnp
from jax import lax
from jax.experimental import pallas as pl
from jax.experimental.pallas import tpu as pltpu
from jax.sharding import PartitionSpec as P

SPAN = 2
RIM = 2


def shifted(value, axis, by):
    length = lax.axis_size(axis)
    return lax.ppermute(value, axis, [(i, (i + by) % length) for i in range(length)])


def with_halo(block, sides, width):
    for axis, dim in sides:
        count = lax.axis_size(axis)
        forward = [(i, i + 1) for i in range(count - 1)]
        backward = [(target, source) for source, target in forward]
        low = lax.ppermute(
            lax.slice_in_dim(block, block.shape[dim] - width, None, axis=dim), axis, forward
        )
        high = lax.ppermute(lax.slice_in_dim(block, 0, width, axis=dim), axis, backward)
        block = jnp.concatenate([low, block, high], axis=dim)
    return block


def masked_taps(lon_taps, lon_width):
    length = lon_taps.shape[2]
    middle = (length - 1) // 2
    distance = jnp.abs(jnp.arange(length, dtype=jnp.int32) - middle)
    keep = distance[None, None, :] <= lon_width[:, None, None]
    return jnp.where(keep, lon_taps, 0.0).astype(jnp.bfloat16)


def longitude_halo(source):
    west = shifted(source, "lon", 1)
    east = shifted(source, "lon", -1)
    far_west = shifted(west, "lon", 1)
    far_east = shifted(east, "lon", -1)
    return far_west, west, east, far_east


def coupling(out_rows, in_rows, basis, valid, output_rows, input_rows, kinds):
    out_match = (out_rows[:, None] == jnp.arange(output_rows, dtype=jnp.int32)[None, :]) & valid[
        :, None
    ]
    in_match = (basis * input_rows + in_rows)[:, None] == jnp.arange(
        kinds * input_rows, dtype=jnp.int32
    )[None, :]
    table = jnp.dot(
        out_match.astype(jnp.float32).T,
        in_match.astype(jnp.float32),
        precision=lax.Precision.HIGHEST,
    )
    return table.reshape(output_rows, kinds, input_rows)


def _toeplitz_kernel(taps_ref, out_ref):
    kinds = taps_ref.shape[1]
    cols = out_ref.shape[2]
    for kind in range(kinds):
        row = taps_ref[0, kind : kind + 1, :]
        wide = jnp.broadcast_to(row, (cols, row.shape[1]))
        out_ref[0, kind] = pltpu.roll(wide, 0, 1, stride=1, stride_axis=0).astype(out_ref.dtype)


def band_matrix(short_taps, cols, window):
    rows, kinds, length = short_taps.shape
    padded = jnp.pad(short_taps.astype(jnp.float32), ((0, 0), (0, 0), (0, window - length)))
    return pl.pallas_call(
        _toeplitz_kernel,
        grid=(rows,),
        in_specs=[pl.BlockSpec((1, kinds, window), lambda i: (i, 0, 0))],
        out_specs=pl.BlockSpec((1, kinds, cols, window), lambda i: (i, 0, 0, 0)),
        out_shape=jax.ShapeDtypeStruct((rows, kinds, cols, window), jnp.bfloat16),
    )(padded)


def _block_kernel(counts_ref, band_ref, far_west_ref, west_ref, local_ref, east_ref, far_east_ref,
                  weight_ref, upper_ref, lower_ref, inner_ref, window_ref, response_ref, mixed_ref, total_ref):
    kind = pl.program_id(0)
    kinds = pl.num_programs(0)
    input_rows, cols, _ = local_ref.shape
    output_rows = input_rows + 2 * RIM
    parts = (far_west_ref, west_ref, local_ref, east_ref, far_east_ref)

    @pl.when(kind == 0)
    def _():
        for index, part in enumerate(parts):
            window_ref[:, index * cols : (index + 1) * cols, :] = part[...]
        total_ref[...] = jnp.zeros_like(total_ref)

    for in_row in range(input_rows):
        response = jnp.dot(band_ref[in_row, 0], window_ref[in_row], preferred_element_type=jnp.float32)
        response_ref[in_row * cols : (in_row + 1) * cols, :] = response.astype(jnp.bfloat16)
    mixed_ref[...] = jnp.dot(response_ref[...], weight_ref[0], preferred_element_type=jnp.float32)
    chunk = 16

    def body(step, carry):
        start = pl.multiple_of(step * chunk, chunk)
        pieces = [mixed_ref[pl.ds(in_row * cols + start, chunk), :] for in_row in range(input_rows)]
        for out_row in range(output_rows):
            total = total_ref[out_row, pl.ds(start, chunk), :]
            for in_row in range(max(0, out_row - 2 * RIM), min(input_rows, out_row + 1)):
                scale = counts_ref[(out_row * kinds + kind) * input_rows + in_row]
                total = total + scale * pieces[in_row]
            total_ref[out_row, pl.ds(start, chunk), :] = total
        return carry

    lax.fori_loop(0, cols // chunk, body, 0)

    @pl.when(kind == kinds - 1)
    def _():
        inner_ref[...] = total_ref[RIM : RIM + input_rows]
        upper_ref[...] = total_ref[:RIM].astype(upper_ref.dtype)
        lower_ref[...] = total_ref[RIM + input_rows :].astype(lower_ref.dtype)


def block_partials(counts, short_taps, parts, mix_weight):
    rows, cols, channels = parts[0].shape
    kinds = short_taps.shape[1]
    window = cols * len(parts)
    band = band_matrix(short_taps, cols, window)
    whole = lambda shape: pl.BlockSpec(shape, lambda k: (0,) * len(shape))
    return pl.pallas_call(
        _block_kernel,
        grid=(kinds,),
        in_specs=[
            pl.BlockSpec(memory_space=pltpu.SMEM),
            pl.BlockSpec((rows, 1, cols, window), lambda k: (0, k, 0, 0)),
        ]
        + [whole(parts[0].shape)] * len(parts)
        + [pl.BlockSpec((1,) + mix_weight.shape[1:], lambda k: (k, 0, 0))],
        out_specs=[whole((RIM, cols, channels))] * 2 + [whole((rows, cols, channels))],
        out_shape=[
            jax.ShapeDtypeStruct((RIM, cols, channels), jnp.bfloat16),
            jax.ShapeDtypeStruct((RIM, cols, channels), jnp.bfloat16),
            jax.ShapeDtypeStruct((rows, cols, channels), jnp.float32),
        ],
        scratch_shapes=[
            pltpu.VMEM((rows, window, channels), jnp.bfloat16),
            pltpu.VMEM((rows * cols, channels), jnp.bfloat16),
            pltpu.VMEM((rows * cols, mix_weight.shape[2]), jnp.float32),
            pltpu.VMEM((rows + 2 * RIM, cols, mix_weight.shape[2]), jnp.float32),
        ],
        compiler_params=pltpu.CompilerParams(dimension_semantics=("arbitrary",)),
    )(counts.reshape(-1), band, *parts, mix_weight)


def on_device(field, lon_width, lon_taps, row_scale, support, mix_weight):
    rows = field.shape[0]
    kinds = lon_taps.shape[1]
    far_west, west, east, far_east = longitude_halo(field)
    short_taps = masked_taps(lon_taps, lon_width)
    entries = support.shape[0]
    lists = with_halo(support, (("lat", 0),), entries)
    above = lists[:entries]
    below = lists[2 * entries :]
    out_rows = jnp.concatenate(
        [support[:, 0] + RIM, above[:, 0] - rows + RIM, below[:, 0] + rows + RIM]
    )
    in_rows = jnp.concatenate([support[:, 1], above[:, 1] - rows, below[:, 1] + rows])
    basis = jnp.concatenate([support[:, 2], above[:, 2], below[:, 2]])
    valid = jnp.concatenate(
        [(support[:, 1] >= 0) & (support[:, 1] < rows), above[:, 1] >= rows, below[:, 1] < 0]
    )
    counts = coupling(out_rows, in_rows, basis, valid, rows + 2 * RIM, rows, kinds)
    upper, lower, inner = block_partials(
        counts, short_taps, (far_west, west, field, east, far_east), mix_weight
    )
    count = lax.axis_size("lat")
    forward = [(i, i + 1) for i in range(count - 1)]
    backward = [(target, source) for source, target in forward]
    from_below = lax.ppermute(upper, "lat", backward).astype(jnp.float32)
    from_above = lax.ppermute(lower, "lat", forward).astype(jnp.float32)
    inner = inner + jnp.pad(from_above, ((0, rows - RIM), (0, 0), (0, 0)))
    inner = inner + jnp.pad(from_below, ((rows - RIM, 0), (0, 0), (0, 0)))
    return (inner * row_scale[:, None, None]).astype(jnp.bfloat16)


def solution(mesh):
    in_specs = (
        P("lat", "lon", None),
        P("lat"),
        P("lat", None, None),
        P("lat"),
        P("lat", None),
        P(),
    )
    out_specs = P("lat", "lon", None)
    return jax.shard_map(
        on_device, mesh=mesh, in_specs=in_specs, out_specs=out_specs, check_vma=False
    )
```

```python
import jax
import jax.numpy as jnp
from jax import lax
from jax.experimental import pallas as pl
from jax.experimental.pallas import tpu as pltpu
from jax.sharding import PartitionSpec as P

SPAN = 2
RIM = 2


def shifted(value, axis, by):
    length = lax.axis_size(axis)
    return lax.ppermute(value, axis, [(i, (i + by) % length) for i in range(length)])


def with_halo(block, sides, width):
    for axis, dim in sides:
        count = lax.axis_size(axis)
        forward = [(i, i + 1) for i in range(count - 1)]
        backward = [(target, source) for source, target in forward]
        low = lax.ppermute(
            lax.slice_in_dim(block, block.shape[dim] - width, None, axis=dim), axis, forward
        )
        high = lax.ppermute(lax.slice_in_dim(block, 0, width, axis=dim), axis, backward)
        block = jnp.concatenate([low, block, high], axis=dim)
    return block


def masked_taps(lon_taps, lon_width):
    length = lon_taps.shape[2]
    middle = (length - 1) // 2
    distance = jnp.abs(jnp.arange(length, dtype=jnp.int32) - middle)
    keep = distance[None, None, :] <= lon_width[:, None, None]
    return jnp.where(keep, lon_taps, 0.0).astype(jnp.bfloat16)


def longitude_halo(source):
    west = shifted(source, "lon", 1)
    east = shifted(source, "lon", -1)
    far_west = shifted(west, "lon", 1)
    far_east = shifted(east, "lon", -1)
    return far_west, west, east, far_east


def coupling(out_rows, in_rows, basis, valid, output_rows, input_rows, kinds):
    out_match = (out_rows[:, None] == jnp.arange(output_rows, dtype=jnp.int32)[None, :]) & valid[
        :, None
    ]
    in_match = (basis * input_rows + in_rows)[:, None] == jnp.arange(
        kinds * input_rows, dtype=jnp.int32
    )[None, :]
    table = jnp.dot(
        out_match.astype(jnp.float32).T,
        in_match.astype(jnp.float32),
        precision=lax.Precision.HIGHEST,
    )
    return table.reshape(output_rows, kinds, input_rows)


def _toeplitz_kernel(taps_ref, out_ref):
    kinds = taps_ref.shape[1]
    cols = out_ref.shape[2]
    for kind in range(kinds):
        row = taps_ref[0, kind : kind + 1, :]
        wide = jnp.broadcast_to(row, (cols, row.shape[1]))
        out_ref[0, kind] = pltpu.roll(wide, 0, 1, stride=1, stride_axis=0).astype(out_ref.dtype)


def band_matrix(short_taps, cols, window):
    rows, kinds, length = short_taps.shape
    padded = jnp.pad(short_taps.astype(jnp.float32), ((0, 0), (0, 0), (0, window - length)))
    return pl.pallas_call(
        _toeplitz_kernel,
        grid=(rows,),
        in_specs=[pl.BlockSpec((1, kinds, window), lambda i: (i, 0, 0))],
        out_specs=pl.BlockSpec((1, kinds, cols, window), lambda i: (i, 0, 0, 0)),
        out_shape=jax.ShapeDtypeStruct((rows, kinds, cols, window), jnp.bfloat16),
    )(padded)


def _block_kernel(counts_ref, band_ref, far_west_ref, west_ref, local_ref, east_ref, far_east_ref,
                  weight_ref, upper_ref, lower_ref, inner_ref, window_ref, response_ref, mixed_ref, total_ref):
    kind = pl.program_id(0)
    kinds = pl.num_programs(0)
    input_rows, cols, _ = local_ref.shape
    output_rows = input_rows + 2 * RIM
    parts = (far_west_ref, west_ref, local_ref, east_ref, far_east_ref)

    @pl.when(kind == 0)
    def _():
        for index, part in enumerate(parts):
            window_ref[:, index * cols : (index + 1) * cols, :] = part[...]
        total_ref[...] = jnp.zeros_like(total_ref)

    for in_row in range(input_rows):
        response = jnp.dot(band_ref[in_row, 0], window_ref[in_row], preferred_element_type=jnp.float32)
        response_ref[in_row * cols : (in_row + 1) * cols, :] = response.astype(jnp.bfloat16)
    mixed_ref[...] = jnp.dot(response_ref[...], weight_ref[0], preferred_element_type=jnp.float32)
    chunk = 16

    def body(step, carry):
        start = pl.multiple_of(step * chunk, chunk)
        pieces = [mixed_ref[pl.ds(in_row * cols + start, chunk), :] for in_row in range(input_rows)]
        for out_row in range(output_rows):
            total = total_ref[out_row, pl.ds(start, chunk), :]
            for in_row in range(max(0, out_row - 2 * RIM), min(input_rows, out_row + 1)):
                scale = counts_ref[(out_row * kinds + kind) * input_rows + in_row]
                total = total + scale * pieces[in_row]
            total_ref[out_row, pl.ds(start, chunk), :] = total
        return carry

    lax.fori_loop(0, cols // chunk, body, 0)

    @pl.when(kind == kinds - 1)
    def _():
        inner_ref[...] = total_ref[RIM : RIM + input_rows]
        upper_ref[...] = total_ref[:RIM].astype(upper_ref.dtype)
        lower_ref[...] = total_ref[RIM + input_rows :].astype(lower_ref.dtype)


def block_partials(counts, band, parts, mix_weight):
    rows, cols, channels = parts[0].shape
    kinds = band.shape[1]
    window = cols * len(parts)
    whole = lambda shape: pl.BlockSpec(shape, lambda k: (0,) * len(shape))
    return pl.pallas_call(
        _block_kernel,
        grid=(kinds,),
        in_specs=[
            pl.BlockSpec(memory_space=pltpu.SMEM),
            pl.BlockSpec((rows, 1, cols, window), lambda k: (0, k, 0, 0)),
        ]
        + [whole(parts[0].shape)] * len(parts)
        + [pl.BlockSpec((1,) + mix_weight.shape[1:], lambda k: (k, 0, 0))],
        out_specs=[whole((RIM, cols, channels))] * 2 + [whole((rows, cols, channels))],
        out_shape=[
            jax.ShapeDtypeStruct((RIM, cols, channels), jnp.bfloat16),
            jax.ShapeDtypeStruct((RIM, cols, channels), jnp.bfloat16),
            jax.ShapeDtypeStruct((rows, cols, channels), jnp.float32),
        ],
        scratch_shapes=[
            pltpu.VMEM((rows, window, channels), jnp.bfloat16),
            pltpu.VMEM((rows * cols, channels), jnp.bfloat16),
            pltpu.VMEM((rows * cols, mix_weight.shape[2]), jnp.float32),
            pltpu.VMEM((rows + 2 * RIM, cols, mix_weight.shape[2]), jnp.float32),
        ],
        compiler_params=pltpu.CompilerParams(dimension_semantics=("arbitrary",)),
    )(counts.reshape(-1), band, *parts, mix_weight)


def on_device(field, lon_width, lon_taps, row_scale, support, mix_weight):
    rows = field.shape[0]
    kinds = lon_taps.shape[1]
    far_west, west, east, far_east = longitude_halo(field)
    short_taps = masked_taps(lon_taps, lon_width)
    cols = field.shape[1]
    band = band_matrix(short_taps, cols, cols * (2 * SPAN + 1))
    band, support = lax.optimization_barrier((band, support))
    entries = support.shape[0]
    lists = with_halo(support, (("lat", 0),), entries)
    above = lists[:entries]
    below = lists[2 * entries :]
    out_rows = jnp.concatenate(
        [support[:, 0] + RIM, above[:, 0] - rows + RIM, below[:, 0] + rows + RIM]
    )
    in_rows = jnp.concatenate([support[:, 1], above[:, 1] - rows, below[:, 1] + rows])
    basis = jnp.concatenate([support[:, 2], above[:, 2], below[:, 2]])
    valid = jnp.concatenate(
        [(support[:, 1] >= 0) & (support[:, 1] < rows), above[:, 1] >= rows, below[:, 1] < 0]
    )
    counts = coupling(out_rows, in_rows, basis, valid, rows + 2 * RIM, rows, kinds)
    upper, lower, inner = block_partials(
        counts, band, (far_west, west, field, east, far_east), mix_weight
    )
    count = lax.axis_size("lat")
    forward = [(i, i + 1) for i in range(count - 1)]
    backward = [(target, source) for source, target in forward]
    from_below = lax.ppermute(upper, "lat", backward).astype(jnp.float32)
    from_above = lax.ppermute(lower, "lat", forward).astype(jnp.float32)
    inner = inner + jnp.pad(from_above, ((0, rows - RIM), (0, 0), (0, 0)))
    inner = inner + jnp.pad(from_below, ((rows - RIM, 0), (0, 0), (0, 0)))
    return (inner * row_scale[:, None, None]).astype(jnp.bfloat16)


def solution(mesh):
    in_specs = (
        P("lat", "lon", None),
        P("lat"),
        P("lat", None, None),
        P("lat"),
        P("lat", None),
        P(),
    )
    out_specs = P("lat", "lon", None)
    return jax.shard_map(
        on_device, mesh=mesh, in_specs=in_specs, out_specs=out_specs, check_vma=False
    )
```

```python
import jax
import jax.numpy as jnp
from jax import lax
from jax.experimental import pallas as pl
from jax.experimental.pallas import tpu as pltpu
from jax.sharding import PartitionSpec as P

SPAN = 2
RIM = 2


def shifted(value, axis, by):
    length = lax.axis_size(axis)
    return lax.ppermute(value, axis, [(i, (i + by) % length) for i in range(length)])


def with_halo(block, sides, width):
    for axis, dim in sides:
        count = lax.axis_size(axis)
        forward = [(i, i + 1) for i in range(count - 1)]
        backward = [(target, source) for source, target in forward]
        low = lax.ppermute(
            lax.slice_in_dim(block, block.shape[dim] - width, None, axis=dim), axis, forward
        )
        high = lax.ppermute(lax.slice_in_dim(block, 0, width, axis=dim), axis, backward)
        block = jnp.concatenate([low, block, high], axis=dim)
    return block


def masked_taps(lon_taps, lon_width):
    length = lon_taps.shape[2]
    middle = (length - 1) // 2
    distance = jnp.abs(jnp.arange(length, dtype=jnp.int32) - middle)
    keep = distance[None, None, :] <= lon_width[:, None, None]
    return jnp.where(keep, lon_taps, 0.0).astype(jnp.bfloat16)


def longitude_halo(source):
    west = shifted(source, "lon", 1)
    east = shifted(source, "lon", -1)
    far_west = shifted(west, "lon", 1)
    far_east = shifted(east, "lon", -1)
    return far_west, west, east, far_east


def coupling(out_rows, in_rows, basis, valid, output_rows, input_rows, kinds):
    out_match = (out_rows[:, None] == jnp.arange(output_rows, dtype=jnp.int32)[None, :]) & valid[
        :, None
    ]
    in_match = (basis * input_rows + in_rows)[:, None] == jnp.arange(
        kinds * input_rows, dtype=jnp.int32
    )[None, :]
    table = jnp.dot(
        out_match.astype(jnp.float32).T,
        in_match.astype(jnp.float32),
        precision=lax.Precision.HIGHEST,
    )
    return table.reshape(output_rows, kinds, input_rows)


def _toeplitz_kernel(taps_ref, out_ref):
    kinds = taps_ref.shape[1]
    cols = out_ref.shape[2]
    for kind in range(kinds):
        row = taps_ref[0, kind : kind + 1, :]
        wide = jnp.broadcast_to(row, (cols, row.shape[1]))
        out_ref[0, kind] = pltpu.roll(wide, 0, 1, stride=1, stride_axis=0).astype(out_ref.dtype)


def band_matrix(short_taps, cols, window):
    rows, kinds, length = short_taps.shape
    padded = jnp.pad(short_taps.astype(jnp.float32), ((0, 0), (0, 0), (0, window - length)))
    return pl.pallas_call(
        _toeplitz_kernel,
        grid=(rows,),
        in_specs=[pl.BlockSpec((1, kinds, window), lambda i: (i, 0, 0))],
        out_specs=pl.BlockSpec((1, kinds, cols, window), lambda i: (i, 0, 0, 0)),
        out_shape=jax.ShapeDtypeStruct((rows, kinds, cols, window), jnp.bfloat16),
    )(padded)


def _block_kernel(counts_ref, band_ref, far_west_ref, west_ref, local_ref, east_ref, far_east_ref,
                  weight_ref, upper_ref, lower_ref, inner_ref, window_ref, response_ref, mixed_ref, total_ref):
    kind = pl.program_id(0)
    kinds = pl.num_programs(0)
    input_rows, cols, _ = local_ref.shape
    output_rows = input_rows + 2 * RIM
    parts = (far_west_ref, west_ref, local_ref, east_ref, far_east_ref)

    @pl.when(kind == 0)
    def _():
        for index, part in enumerate(parts):
            window_ref[:, index * cols : (index + 1) * cols, :] = part[...]

    for in_row in range(input_rows):
        response = jnp.dot(band_ref[in_row, 0], window_ref[in_row], preferred_element_type=jnp.float32)
        response_ref[in_row * cols : (in_row + 1) * cols, :] = response.astype(jnp.bfloat16)
    mixed_ref[...] = jnp.dot(response_ref[...], weight_ref[0], preferred_element_type=jnp.float32)
    chunk = 16

    def accumulate(first):
        def body(step, carry):
            start = pl.multiple_of(step * chunk, chunk)
            pieces = [mixed_ref[pl.ds(in_row * cols + start, chunk), :] for in_row in range(input_rows)]
            for out_row in range(output_rows):
                total = None if first else total_ref[out_row, pl.ds(start, chunk), :]
                for in_row in range(max(0, out_row - 2 * RIM), min(input_rows, out_row + 1)):
                    scale = counts_ref[(out_row * kinds + kind) * input_rows + in_row]
                    term = scale * pieces[in_row]
                    total = term if total is None else total + term
                total_ref[out_row, pl.ds(start, chunk), :] = total
            return carry

        lax.fori_loop(0, cols // chunk, body, 0)

    pl.when(kind == 0)(lambda: accumulate(True))
    pl.when(kind > 0)(lambda: accumulate(False))

    @pl.when(kind == kinds - 1)
    def _():
        inner_ref[...] = total_ref[RIM : RIM + input_rows]
        upper_ref[...] = total_ref[:RIM].astype(upper_ref.dtype)
        lower_ref[...] = total_ref[RIM + input_rows :].astype(lower_ref.dtype)


def block_partials(counts, short_taps, parts, mix_weight):
    rows, cols, channels = parts[0].shape
    kinds = short_taps.shape[1]
    window = cols * len(parts)
    band = band_matrix(short_taps, cols, window)
    whole = lambda shape: pl.BlockSpec(shape, lambda k: (0,) * len(shape))
    return pl.pallas_call(
        _block_kernel,
        grid=(kinds,),
        in_specs=[
            pl.BlockSpec(memory_space=pltpu.SMEM),
            pl.BlockSpec((rows, 1, cols, window), lambda k: (0, k, 0, 0)),
        ]
        + [whole(parts[0].shape)] * len(parts)
        + [pl.BlockSpec((1,) + mix_weight.shape[1:], lambda k: (k, 0, 0))],
        out_specs=[whole((RIM, cols, channels))] * 2 + [whole((rows, cols, channels))],
        out_shape=[
            jax.ShapeDtypeStruct((RIM, cols, channels), jnp.bfloat16),
            jax.ShapeDtypeStruct((RIM, cols, channels), jnp.bfloat16),
            jax.ShapeDtypeStruct((rows, cols, channels), jnp.float32),
        ],
        scratch_shapes=[
            pltpu.VMEM((rows, window, channels), jnp.bfloat16),
            pltpu.VMEM((rows * cols, channels), jnp.bfloat16),
            pltpu.VMEM((rows * cols, mix_weight.shape[2]), jnp.float32),
            pltpu.VMEM((rows + 2 * RIM, cols, mix_weight.shape[2]), jnp.float32),
        ],
        compiler_params=pltpu.CompilerParams(dimension_semantics=("arbitrary",)),
    )(counts.reshape(-1), band, *parts, mix_weight)


def on_device(field, lon_width, lon_taps, row_scale, support, mix_weight):
    rows = field.shape[0]
    kinds = lon_taps.shape[1]
    far_west, west, east, far_east = longitude_halo(field)
    short_taps = masked_taps(lon_taps, lon_width)
    entries = support.shape[0]
    lists = with_halo(support, (("lat", 0),), entries)
    above = lists[:entries]
    below = lists[2 * entries :]
    out_rows = jnp.concatenate(
        [support[:, 0] + RIM, above[:, 0] - rows + RIM, below[:, 0] + rows + RIM]
    )
    in_rows = jnp.concatenate([support[:, 1], above[:, 1] - rows, below[:, 1] + rows])
    basis = jnp.concatenate([support[:, 2], above[:, 2], below[:, 2]])
    valid = jnp.concatenate(
        [(support[:, 1] >= 0) & (support[:, 1] < rows), above[:, 1] >= rows, below[:, 1] < 0]
    )
    counts = coupling(out_rows, in_rows, basis, valid, rows + 2 * RIM, rows, kinds)
    upper, lower, inner = block_partials(
        counts, short_taps, (far_west, west, field, east, far_east), mix_weight
    )
    count = lax.axis_size("lat")
    forward = [(i, i + 1) for i in range(count - 1)]
    backward = [(target, source) for source, target in forward]
    from_below = lax.ppermute(upper, "lat", backward).astype(jnp.float32)
    from_above = lax.ppermute(lower, "lat", forward).astype(jnp.float32)
    inner = inner + jnp.pad(from_above, ((0, rows - RIM), (0, 0), (0, 0)))
    inner = inner + jnp.pad(from_below, ((rows - RIM, 0), (0, 0), (0, 0)))
    return (inner * row_scale[:, None, None]).astype(jnp.bfloat16)


def solution(mesh):
    in_specs = (
        P("lat", "lon", None),
        P("lat"),
        P("lat", None, None),
        P("lat"),
        P("lat", None),
        P(),
    )
    out_specs = P("lat", "lon", None)
    return jax.shard_map(
        on_device, mesh=mesh, in_specs=in_specs, out_specs=out_specs, check_vma=False
    )
```

```python
import jax
import jax.numpy as jnp
from jax import lax
from jax.experimental import pallas as pl
from jax.experimental.pallas import tpu as pltpu
from jax.sharding import PartitionSpec as P

SPAN = 2
RIM = 2


def shifted(value, axis, by):
    length = lax.axis_size(axis)
    return lax.ppermute(value, axis, [(i, (i + by) % length) for i in range(length)])


def with_halo(block, sides, width):
    for axis, dim in sides:
        count = lax.axis_size(axis)
        forward = [(i, i + 1) for i in range(count - 1)]
        backward = [(target, source) for source, target in forward]
        low = lax.ppermute(
            lax.slice_in_dim(block, block.shape[dim] - width, None, axis=dim), axis, forward
        )
        high = lax.ppermute(lax.slice_in_dim(block, 0, width, axis=dim), axis, backward)
        block = jnp.concatenate([low, block, high], axis=dim)
    return block


def masked_taps(lon_taps, lon_width):
    length = lon_taps.shape[2]
    middle = (length - 1) // 2
    distance = jnp.abs(jnp.arange(length, dtype=jnp.int32) - middle)
    keep = distance[None, None, :] <= lon_width[:, None, None]
    return jnp.where(keep, lon_taps, 0.0).astype(jnp.bfloat16)


def longitude_halo(source):
    west = shifted(source, "lon", 1)
    east = shifted(source, "lon", -1)
    far_west = shifted(west, "lon", 1)
    far_east = shifted(east, "lon", -1)
    return far_west, west, east, far_east


def coupling(out_rows, in_rows, basis, valid, output_rows, input_rows, kinds):
    out_match = (out_rows[:, None] == jnp.arange(output_rows, dtype=jnp.int32)[None, :]) & valid[
        :, None
    ]
    in_match = (basis * input_rows + in_rows)[:, None] == jnp.arange(
        kinds * input_rows, dtype=jnp.int32
    )[None, :]
    table = jnp.dot(
        out_match.astype(jnp.float32).T,
        in_match.astype(jnp.float32),
        precision=lax.Precision.HIGHEST,
    )
    return table.reshape(output_rows, kinds, input_rows)


def _toeplitz_kernel(taps_ref, out_ref):
    kinds = taps_ref.shape[1]
    cols = out_ref.shape[2]
    for kind in range(kinds):
        row = taps_ref[0, kind : kind + 1, :]
        wide = jnp.broadcast_to(row, (cols, row.shape[1]))
        out_ref[0, kind] = pltpu.roll(wide, 0, 1, stride=1, stride_axis=0).astype(out_ref.dtype)


def band_matrix(short_taps, cols, window):
    rows, kinds, length = short_taps.shape
    padded = jnp.pad(short_taps.astype(jnp.float32), ((0, 0), (0, 0), (0, window - length)))
    return pl.pallas_call(
        _toeplitz_kernel,
        grid=(rows,),
        in_specs=[pl.BlockSpec((1, kinds, window), lambda i: (i, 0, 0))],
        out_specs=pl.BlockSpec((1, kinds, cols, window), lambda i: (i, 0, 0, 0)),
        out_shape=jax.ShapeDtypeStruct((rows, kinds, cols, window), jnp.bfloat16),
    )(padded)


def _block_kernel(counts_ref, band_ref, far_west_ref, west_ref, local_ref, east_ref, far_east_ref,
                  weight_ref, upper_ref, lower_ref, inner_ref, window_ref, response_ref, mixed_ref, total_ref):
    kind = pl.program_id(0)
    kinds = pl.num_programs(0)
    input_rows, cols, _ = local_ref.shape
    output_rows = input_rows + 2 * RIM
    parts = (far_west_ref, west_ref, local_ref, east_ref, far_east_ref)

    @pl.when(kind == 0)
    def _():
        for index, part in enumerate(parts):
            window_ref[:, index * cols : (index + 1) * cols, :] = part[...]

    for in_row in range(input_rows):
        response = jnp.dot(band_ref[in_row, 0], window_ref[in_row], preferred_element_type=jnp.float32)
        response_ref[in_row * cols : (in_row + 1) * cols, :] = response.astype(jnp.bfloat16)
    mixed_ref[...] = jnp.dot(response_ref[...], weight_ref[0], preferred_element_type=jnp.float32)
    chunk = 16

    def accumulate(first, last):
        def body(step, carry):
            start = pl.multiple_of(step * chunk, chunk)
            pieces = [mixed_ref[pl.ds(in_row * cols + start, chunk), :] for in_row in range(input_rows)]
            for out_row in range(output_rows):
                total = None if first else total_ref[out_row, pl.ds(start, chunk), :]
                for in_row in range(max(0, out_row - 2 * RIM), min(input_rows, out_row + 1)):
                    scale = counts_ref[(out_row * kinds + kind) * input_rows + in_row]
                    term = scale * pieces[in_row]
                    total = term if total is None else total + term
                if not last:
                    total_ref[out_row, pl.ds(start, chunk), :] = total
                elif out_row < RIM:
                    upper_ref[out_row, pl.ds(start, chunk), :] = total.astype(upper_ref.dtype)
                elif out_row < RIM + input_rows:
                    inner_ref[out_row - RIM, pl.ds(start, chunk), :] = total
                else:
                    lower_ref[out_row - RIM - input_rows, pl.ds(start, chunk), :] = total.astype(lower_ref.dtype)
            return carry

        lax.fori_loop(0, cols // chunk, body, 0)

    pl.when(kind == 0)(lambda: accumulate(True, False))
    pl.when((kind > 0) & (kind < kinds - 1))(lambda: accumulate(False, False))
    pl.when(kind == kinds - 1)(lambda: accumulate(False, True))


def block_partials(counts, short_taps, parts, mix_weight):
    rows, cols, channels = parts[0].shape
    kinds = short_taps.shape[1]
    window = cols * len(parts)
    band = band_matrix(short_taps, cols, window)
    whole = lambda shape: pl.BlockSpec(shape, lambda k: (0,) * len(shape))
    return pl.pallas_call(
        _block_kernel,
        grid=(kinds,),
        in_specs=[
            pl.BlockSpec(memory_space=pltpu.SMEM),
            pl.BlockSpec((rows, 1, cols, window), lambda k: (0, k, 0, 0)),
        ]
        + [whole(parts[0].shape)] * len(parts)
        + [pl.BlockSpec((1,) + mix_weight.shape[1:], lambda k: (k, 0, 0))],
        out_specs=[whole((RIM, cols, channels))] * 2 + [whole((rows, cols, channels))],
        out_shape=[
            jax.ShapeDtypeStruct((RIM, cols, channels), jnp.bfloat16),
            jax.ShapeDtypeStruct((RIM, cols, channels), jnp.bfloat16),
            jax.ShapeDtypeStruct((rows, cols, channels), jnp.float32),
        ],
        scratch_shapes=[
            pltpu.VMEM((rows, window, channels), jnp.bfloat16),
            pltpu.VMEM((rows * cols, channels), jnp.bfloat16),
            pltpu.VMEM((rows * cols, mix_weight.shape[2]), jnp.float32),
            pltpu.VMEM((rows + 2 * RIM, cols, mix_weight.shape[2]), jnp.float32),
        ],
        compiler_params=pltpu.CompilerParams(dimension_semantics=("arbitrary",)),
    )(counts.reshape(-1), band, *parts, mix_weight)


def on_device(field, lon_width, lon_taps, row_scale, support, mix_weight):
    rows = field.shape[0]
    kinds = lon_taps.shape[1]
    far_west, west, east, far_east = longitude_halo(field)
    short_taps = masked_taps(lon_taps, lon_width)
    entries = support.shape[0]
    lists = with_halo(support, (("lat", 0),), entries)
    above = lists[:entries]
    below = lists[2 * entries :]
    out_rows = jnp.concatenate(
        [support[:, 0] + RIM, above[:, 0] - rows + RIM, below[:, 0] + rows + RIM]
    )
    in_rows = jnp.concatenate([support[:, 1], above[:, 1] - rows, below[:, 1] + rows])
    basis = jnp.concatenate([support[:, 2], above[:, 2], below[:, 2]])
    valid = jnp.concatenate(
        [(support[:, 1] >= 0) & (support[:, 1] < rows), above[:, 1] >= rows, below[:, 1] < 0]
    )
    counts = coupling(out_rows, in_rows, basis, valid, rows + 2 * RIM, rows, kinds)
    upper, lower, inner = block_partials(
        counts, short_taps, (far_west, west, field, east, far_east), mix_weight
    )
    count = lax.axis_size("lat")
    forward = [(i, i + 1) for i in range(count - 1)]
    backward = [(target, source) for source, target in forward]
    from_below = lax.ppermute(upper, "lat", backward).astype(jnp.float32)
    from_above = lax.ppermute(lower, "lat", forward).astype(jnp.float32)
    inner = inner + jnp.pad(from_above, ((0, rows - RIM), (0, 0), (0, 0)))
    inner = inner + jnp.pad(from_below, ((rows - RIM, 0), (0, 0), (0, 0)))
    return (inner * row_scale[:, None, None]).astype(jnp.bfloat16)


def solution(mesh):
    in_specs = (
        P("lat", "lon", None),
        P("lat"),
        P("lat", None, None),
        P("lat"),
        P("lat", None),
        P(),
    )
    out_specs = P("lat", "lon", None)
    return jax.shard_map(
        on_device, mesh=mesh, in_specs=in_specs, out_specs=out_specs, check_vma=False
    )
```

```python
import jax
import jax.numpy as jnp
from jax import lax
from jax.experimental import pallas as pl
from jax.experimental.pallas import tpu as pltpu
from jax.sharding import PartitionSpec as P

SPAN = 2
RIM = 2


def shifted(value, axis, by):
    length = lax.axis_size(axis)
    return lax.ppermute(value, axis, [(i, (i + by) % length) for i in range(length)])


def with_halo(block, sides, width):
    for axis, dim in sides:
        count = lax.axis_size(axis)
        forward = [(i, i + 1) for i in range(count - 1)]
        backward = [(target, source) for source, target in forward]
        low = lax.ppermute(
            lax.slice_in_dim(block, block.shape[dim] - width, None, axis=dim), axis, forward
        )
        high = lax.ppermute(lax.slice_in_dim(block, 0, width, axis=dim), axis, backward)
        block = jnp.concatenate([low, block, high], axis=dim)
    return block


def masked_taps(lon_taps, lon_width):
    length = lon_taps.shape[2]
    middle = (length - 1) // 2
    distance = jnp.abs(jnp.arange(length, dtype=jnp.int32) - middle)
    keep = distance[None, None, :] <= lon_width[:, None, None]
    return jnp.where(keep, lon_taps, 0.0).astype(jnp.bfloat16)


def longitude_halo(source):
    west = shifted(source, "lon", 1)
    east = shifted(source, "lon", -1)
    far_west = shifted(west, "lon", 1)
    far_east = shifted(east, "lon", -1)
    return far_west, west, east, far_east


def coupling(out_rows, in_rows, basis, valid, output_rows, input_rows, kinds):
    out_match = (out_rows[:, None] == jnp.arange(output_rows, dtype=jnp.int32)[None, :]) & valid[
        :, None
    ]
    in_match = (basis * input_rows + in_rows)[:, None] == jnp.arange(
        kinds * input_rows, dtype=jnp.int32
    )[None, :]
    table = jnp.dot(
        out_match.astype(jnp.float32).T,
        in_match.astype(jnp.float32),
        precision=lax.Precision.HIGHEST,
    )
    return table.reshape(output_rows, kinds, input_rows)


def _toeplitz_kernel(taps_ref, out_ref):
    kinds = taps_ref.shape[1]
    cols = out_ref.shape[2]
    for kind in range(kinds):
        row = taps_ref[0, kind : kind + 1, :]
        wide = jnp.broadcast_to(row, (cols, row.shape[1]))
        out_ref[0, kind] = pltpu.roll(wide, 0, 1, stride=1, stride_axis=0).astype(out_ref.dtype)


def band_matrix(short_taps, cols, window):
    rows, kinds, length = short_taps.shape
    padded = jnp.pad(short_taps.astype(jnp.float32), ((0, 0), (0, 0), (0, window - length)))
    return pl.pallas_call(
        _toeplitz_kernel,
        grid=(rows,),
        in_specs=[pl.BlockSpec((1, kinds, window), lambda i: (i, 0, 0))],
        out_specs=pl.BlockSpec((1, kinds, cols, window), lambda i: (i, 0, 0, 0)),
        out_shape=jax.ShapeDtypeStruct((rows, kinds, cols, window), jnp.bfloat16),
    )(padded)


def _block_kernel(counts_ref, band_ref, far_west_ref, west_ref, local_ref, east_ref, far_east_ref,
                  weight_ref, upper_ref, lower_ref, inner_ref, response_ref, mixed_ref, total_ref):
    kind = pl.program_id(0)
    kinds = pl.num_programs(0)
    input_rows, cols, _ = local_ref.shape
    output_rows = input_rows + 2 * RIM
    parts = (far_west_ref, west_ref, local_ref, east_ref, far_east_ref)

    for in_row in range(input_rows):
        response = None
        for index, part in enumerate(parts):
            term = jnp.dot(
                band_ref[in_row, 0, :, index * cols : (index + 1) * cols],
                part[in_row],
                preferred_element_type=jnp.float32,
            )
            response = term if response is None else response + term
        response_ref[in_row * cols : (in_row + 1) * cols, :] = response.astype(jnp.bfloat16)
    mixed_ref[...] = jnp.dot(response_ref[...], weight_ref[0], preferred_element_type=jnp.float32)
    chunk = 16

    def accumulate(first):
        def body(step, carry):
            start = pl.multiple_of(step * chunk, chunk)
            pieces = [mixed_ref[pl.ds(in_row * cols + start, chunk), :] for in_row in range(input_rows)]
            for out_row in range(output_rows):
                total = None if first else total_ref[out_row, pl.ds(start, chunk), :]
                for in_row in range(max(0, out_row - 2 * RIM), min(input_rows, out_row + 1)):
                    scale = counts_ref[(out_row * kinds + kind) * input_rows + in_row]
                    term = scale * pieces[in_row]
                    total = term if total is None else total + term
                total_ref[out_row, pl.ds(start, chunk), :] = total
            return carry

        lax.fori_loop(0, cols // chunk, body, 0)

    pl.when(kind == 0)(lambda: accumulate(True))
    pl.when(kind > 0)(lambda: accumulate(False))

    @pl.when(kind == kinds - 1)
    def _():
        inner_ref[...] = total_ref[RIM : RIM + input_rows]
        upper_ref[...] = total_ref[:RIM].astype(upper_ref.dtype)
        lower_ref[...] = total_ref[RIM + input_rows :].astype(lower_ref.dtype)


def block_partials(counts, short_taps, parts, mix_weight):
    rows, cols, channels = parts[0].shape
    kinds = short_taps.shape[1]
    window = cols * len(parts)
    band = band_matrix(short_taps, cols, window)
    whole = lambda shape: pl.BlockSpec(shape, lambda k: (0,) * len(shape))
    return pl.pallas_call(
        _block_kernel,
        grid=(kinds,),
        in_specs=[
            pl.BlockSpec(memory_space=pltpu.SMEM),
            pl.BlockSpec((rows, 1, cols, window), lambda k: (0, k, 0, 0)),
        ]
        + [whole(parts[0].shape)] * len(parts)
        + [pl.BlockSpec((1,) + mix_weight.shape[1:], lambda k: (k, 0, 0))],
        out_specs=[whole((RIM, cols, channels))] * 2 + [whole((rows, cols, channels))],
        out_shape=[
            jax.ShapeDtypeStruct((RIM, cols, channels), jnp.bfloat16),
            jax.ShapeDtypeStruct((RIM, cols, channels), jnp.bfloat16),
            jax.ShapeDtypeStruct((rows, cols, channels), jnp.float32),
        ],
        scratch_shapes=[
            pltpu.VMEM((rows * cols, channels), jnp.bfloat16),
            pltpu.VMEM((rows * cols, mix_weight.shape[2]), jnp.float32),
            pltpu.VMEM((rows + 2 * RIM, cols, mix_weight.shape[2]), jnp.float32),
        ],
        compiler_params=pltpu.CompilerParams(dimension_semantics=("arbitrary",)),
    )(counts.reshape(-1), band, *parts, mix_weight)


def on_device(field, lon_width, lon_taps, row_scale, support, mix_weight):
    rows = field.shape[0]
    kinds = lon_taps.shape[1]
    far_west, west, east, far_east = longitude_halo(field)
    short_taps = masked_taps(lon_taps, lon_width)
    entries = support.shape[0]
    lists = with_halo(support, (("lat", 0),), entries)
    above = lists[:entries]
    below = lists[2 * entries :]
    out_rows = jnp.concatenate(
        [support[:, 0] + RIM, above[:, 0] - rows + RIM, below[:, 0] + rows + RIM]
    )
    in_rows = jnp.concatenate([support[:, 1], above[:, 1] - rows, below[:, 1] + rows])
    basis = jnp.concatenate([support[:, 2], above[:, 2], below[:, 2]])
    valid = jnp.concatenate(
        [(support[:, 1] >= 0) & (support[:, 1] < rows), above[:, 1] >= rows, below[:, 1] < 0]
    )
    counts = coupling(out_rows, in_rows, basis, valid, rows + 2 * RIM, rows, kinds)
    upper, lower, inner = block_partials(
        counts, short_taps, (far_west, west, field, east, far_east), mix_weight
    )
    count = lax.axis_size("lat")
    forward = [(i, i + 1) for i in range(count - 1)]
    backward = [(target, source) for source, target in forward]
    from_below = lax.ppermute(upper, "lat", backward).astype(jnp.float32)
    from_above = lax.ppermute(lower, "lat", forward).astype(jnp.float32)
    inner = inner + jnp.pad(from_above, ((0, rows - RIM), (0, 0), (0, 0)))
    inner = inner + jnp.pad(from_below, ((rows - RIM, 0), (0, 0), (0, 0)))
    return (inner * row_scale[:, None, None]).astype(jnp.bfloat16)


def solution(mesh):
    in_specs = (
        P("lat", "lon", None),
        P("lat"),
        P("lat", None, None),
        P("lat"),
        P("lat", None),
        P(),
    )
    out_specs = P("lat", "lon", None)
    return jax.shard_map(
        on_device, mesh=mesh, in_specs=in_specs, out_specs=out_specs, check_vma=False
    )
```

```python
import jax
import jax.numpy as jnp
from jax import lax
from jax.experimental import pallas as pl
from jax.experimental.pallas import tpu as pltpu
from jax.sharding import PartitionSpec as P

SPAN = 2
RIM = 2


def shifted(value, axis, by):
    length = lax.axis_size(axis)
    return lax.ppermute(value, axis, [(i, (i + by) % length) for i in range(length)])


def with_halo(block, sides, width):
    for axis, dim in sides:
        count = lax.axis_size(axis)
        forward = [(i, i + 1) for i in range(count - 1)]
        backward = [(target, source) for source, target in forward]
        low = lax.ppermute(
            lax.slice_in_dim(block, block.shape[dim] - width, None, axis=dim), axis, forward
        )
        high = lax.ppermute(lax.slice_in_dim(block, 0, width, axis=dim), axis, backward)
        block = jnp.concatenate([low, block, high], axis=dim)
    return block


def masked_taps(lon_taps, lon_width):
    length = lon_taps.shape[2]
    middle = (length - 1) // 2
    distance = jnp.abs(jnp.arange(length, dtype=jnp.int32) - middle)
    keep = distance[None, None, :] <= lon_width[:, None, None]
    return jnp.where(keep, lon_taps, 0.0).astype(jnp.bfloat16)


def longitude_halo(source):
    west = shifted(source, "lon", 1)
    east = shifted(source, "lon", -1)
    far_west = shifted(west, "lon", 1)
    far_east = shifted(east, "lon", -1)
    return far_west, west, east, far_east


def coupling(out_rows, in_rows, basis, valid, output_rows, input_rows, kinds):
    out_match = (out_rows[:, None] == jnp.arange(output_rows, dtype=jnp.int32)[None, :]) & valid[
        :, None
    ]
    in_match = (basis * input_rows + in_rows)[:, None] == jnp.arange(
        kinds * input_rows, dtype=jnp.int32
    )[None, :]
    table = jnp.dot(
        out_match.astype(jnp.float32).T,
        in_match.astype(jnp.float32),
        precision=lax.Precision.HIGHEST,
    )
    return table.reshape(output_rows, kinds, input_rows)


def _toeplitz_kernel(taps_ref, out_ref):
    kinds = taps_ref.shape[1]
    cols = out_ref.shape[2]
    for kind in range(kinds):
        row = taps_ref[0, kind : kind + 1, :]
        wide = jnp.broadcast_to(row, (cols, row.shape[1]))
        out_ref[0, kind] = pltpu.roll(wide, 0, 1, stride=1, stride_axis=0).astype(out_ref.dtype)


def band_matrix(short_taps, cols, window):
    rows, kinds, length = short_taps.shape
    padded = jnp.pad(short_taps.astype(jnp.float32), ((0, 0), (0, 0), (0, window - length)))
    return pl.pallas_call(
        _toeplitz_kernel,
        grid=(rows,),
        in_specs=[pl.BlockSpec((1, kinds, window), lambda i: (i, 0, 0))],
        out_specs=pl.BlockSpec((1, kinds, cols, window), lambda i: (i, 0, 0, 0)),
        out_shape=jax.ShapeDtypeStruct((rows, kinds, cols, window), jnp.bfloat16),
    )(padded)


def _block_kernel(counts_ref, band_ref, far_west_ref, west_ref, local_ref, east_ref, far_east_ref,
                  weight_ref, upper_ref, lower_ref, inner_ref, window_ref, response_ref, mixed_ref, total_ref):
    kind = pl.program_id(0)
    kinds = pl.num_programs(0)
    input_rows, cols, _ = local_ref.shape
    output_rows = input_rows + 2 * RIM
    parts = (far_west_ref, west_ref, local_ref, east_ref, far_east_ref)

    @pl.when(kind == 0)
    def _():
        for index, part in enumerate(parts):
            window_ref[:, index * cols : (index + 1) * cols, :] = part[...]

    for in_row in range(input_rows):
        response = jnp.dot(band_ref[in_row, 0], window_ref[in_row], preferred_element_type=jnp.float32)
        response_ref[in_row * cols : (in_row + 1) * cols, :] = response.astype(jnp.bfloat16)
    mixed_ref[...] = jnp.dot(response_ref[...], weight_ref[0], preferred_element_type=jnp.float32)
    chunk = 32

    def accumulate(first):
        def body(step, carry):
            start = pl.multiple_of(step * chunk, chunk)
            pieces = [mixed_ref[pl.ds(in_row * cols + start, chunk), :] for in_row in range(input_rows)]
            for out_row in range(output_rows):
                total = None if first else total_ref[out_row, pl.ds(start, chunk), :]
                for in_row in range(max(0, out_row - 2 * RIM), min(input_rows, out_row + 1)):
                    scale = counts_ref[(out_row * kinds + kind) * input_rows + in_row]
                    term = scale * pieces[in_row]
                    total = term if total is None else total + term
                total_ref[out_row, pl.ds(start, chunk), :] = total
            return carry

        lax.fori_loop(0, cols // chunk, body, 0)

    pl.when(kind == 0)(lambda: accumulate(True))
    pl.when(kind > 0)(lambda: accumulate(False))

    @pl.when(kind == kinds - 1)
    def _():
        inner_ref[...] = total_ref[RIM : RIM + input_rows]
        upper_ref[...] = total_ref[:RIM].astype(upper_ref.dtype)
        lower_ref[...] = total_ref[RIM + input_rows :].astype(lower_ref.dtype)


def block_partials(counts, short_taps, parts, mix_weight):
    rows, cols, channels = parts[0].shape
    kinds = short_taps.shape[1]
    window = cols * len(parts)
    band = band_matrix(short_taps, cols, window)
    whole = lambda shape: pl.BlockSpec(shape, lambda k: (0,) * len(shape))
    return pl.pallas_call(
        _block_kernel,
        grid=(kinds,),
        in_specs=[
            pl.BlockSpec(memory_space=pltpu.SMEM),
            pl.BlockSpec((rows, 1, cols, window), lambda k: (0, k, 0, 0)),
        ]
        + [whole(parts[0].shape)] * len(parts)
        + [pl.BlockSpec((1,) + mix_weight.shape[1:], lambda k: (k, 0, 0))],
        out_specs=[whole((RIM, cols, channels))] * 2 + [whole((rows, cols, channels))],
        out_shape=[
            jax.ShapeDtypeStruct((RIM, cols, channels), jnp.bfloat16),
            jax.ShapeDtypeStruct((RIM, cols, channels), jnp.bfloat16),
            jax.ShapeDtypeStruct((rows, cols, channels), jnp.float32),
        ],
        scratch_shapes=[
            pltpu.VMEM((rows, window, channels), jnp.bfloat16),
            pltpu.VMEM((rows * cols, channels), jnp.bfloat16),
            pltpu.VMEM((rows * cols, mix_weight.shape[2]), jnp.float32),
            pltpu.VMEM((rows + 2 * RIM, cols, mix_weight.shape[2]), jnp.float32),
        ],
        compiler_params=pltpu.CompilerParams(dimension_semantics=("arbitrary",)),
    )(counts.reshape(-1), band, *parts, mix_weight)


def on_device(field, lon_width, lon_taps, row_scale, support, mix_weight):
    rows = field.shape[0]
    kinds = lon_taps.shape[1]
    far_west, west, east, far_east = longitude_halo(field)
    short_taps = masked_taps(lon_taps, lon_width)
    entries = support.shape[0]
    lists = with_halo(support, (("lat", 0),), entries)
    above = lists[:entries]
    below = lists[2 * entries :]
    out_rows = jnp.concatenate(
        [support[:, 0] + RIM, above[:, 0] - rows + RIM, below[:, 0] + rows + RIM]
    )
    in_rows = jnp.concatenate([support[:, 1], above[:, 1] - rows, below[:, 1] + rows])
    basis = jnp.concatenate([support[:, 2], above[:, 2], below[:, 2]])
    valid = jnp.concatenate(
        [(support[:, 1] >= 0) & (support[:, 1] < rows), above[:, 1] >= rows, below[:, 1] < 0]
    )
    counts = coupling(out_rows, in_rows, basis, valid, rows + 2 * RIM, rows, kinds)
    upper, lower, inner = block_partials(
        counts, short_taps, (far_west, west, field, east, far_east), mix_weight
    )
    count = lax.axis_size("lat")
    forward = [(i, i + 1) for i in range(count - 1)]
    backward = [(target, source) for source, target in forward]
    from_below = lax.ppermute(upper, "lat", backward).astype(jnp.float32)
    from_above = lax.ppermute(lower, "lat", forward).astype(jnp.float32)
    inner = inner + jnp.pad(from_above, ((0, rows - RIM), (0, 0), (0, 0)))
    inner = inner + jnp.pad(from_below, ((rows - RIM, 0), (0, 0), (0, 0)))
    return (inner * row_scale[:, None, None]).astype(jnp.bfloat16)


def solution(mesh):
    in_specs = (
        P("lat", "lon", None),
        P("lat"),
        P("lat", None, None),
        P("lat"),
        P("lat", None),
        P(),
    )
    out_specs = P("lat", "lon", None)
    return jax.shard_map(
        on_device, mesh=mesh, in_specs=in_specs, out_specs=out_specs, check_vma=False
    )
```

```python
import jax
import jax.numpy as jnp
from jax import lax
from jax.experimental import pallas as pl
from jax.experimental.pallas import tpu as pltpu
from jax.sharding import PartitionSpec as P

SPAN = 2
RIM = 2


def shifted(value, axis, by):
    length = lax.axis_size(axis)
    return lax.ppermute(value, axis, [(i, (i + by) % length) for i in range(length)])


def with_halo(block, sides, width):
    for axis, dim in sides:
        count = lax.axis_size(axis)
        forward = [(i, i + 1) for i in range(count - 1)]
        backward = [(target, source) for source, target in forward]
        low = lax.ppermute(
            lax.slice_in_dim(block, block.shape[dim] - width, None, axis=dim), axis, forward
        )
        high = lax.ppermute(lax.slice_in_dim(block, 0, width, axis=dim), axis, backward)
        block = jnp.concatenate([low, block, high], axis=dim)
    return block


def masked_taps(lon_taps, lon_width):
    length = lon_taps.shape[2]
    middle = (length - 1) // 2
    distance = jnp.abs(jnp.arange(length, dtype=jnp.int32) - middle)
    keep = distance[None, None, :] <= lon_width[:, None, None]
    return jnp.where(keep, lon_taps, 0.0).astype(jnp.bfloat16)


def longitude_halo(source):
    west = shifted(source, "lon", 1)
    east = shifted(source, "lon", -1)
    far_west = shifted(west, "lon", 1)
    far_east = shifted(east, "lon", -1)
    return far_west, west, east, far_east


def coupling(out_rows, in_rows, basis, valid, output_rows, input_rows, kinds):
    out_match = (out_rows[:, None] == jnp.arange(output_rows, dtype=jnp.int32)[None, :]) & valid[
        :, None
    ]
    in_match = (basis * input_rows + in_rows)[:, None] == jnp.arange(
        kinds * input_rows, dtype=jnp.int32
    )[None, :]
    table = jnp.dot(
        out_match.astype(jnp.float32).T,
        in_match.astype(jnp.float32),
        precision=lax.Precision.HIGHEST,
    )
    return table.reshape(output_rows, kinds, input_rows)


def _toeplitz_kernel(taps_ref, out_ref):
    kinds = taps_ref.shape[1]
    cols = out_ref.shape[2]
    for kind in range(kinds):
        row = taps_ref[0, kind : kind + 1, :]
        wide = jnp.broadcast_to(row, (cols, row.shape[1]))
        out_ref[0, kind] = pltpu.roll(wide, 0, 1, stride=1, stride_axis=0).astype(out_ref.dtype)


def band_matrix(short_taps, cols, window):
    rows, kinds, length = short_taps.shape
    padded = jnp.pad(short_taps.astype(jnp.float32), ((0, 0), (0, 0), (0, window - length)))
    return pl.pallas_call(
        _toeplitz_kernel,
        grid=(rows,),
        in_specs=[pl.BlockSpec((1, kinds, window), lambda i: (i, 0, 0))],
        out_specs=pl.BlockSpec((1, kinds, cols, window), lambda i: (i, 0, 0, 0)),
        out_shape=jax.ShapeDtypeStruct((rows, kinds, cols, window), jnp.bfloat16),
    )(padded)


def _block_kernel(counts_ref, band_ref, far_west_ref, west_ref, local_ref, east_ref, far_east_ref,
                  weight_ref, upper_ref, lower_ref, inner_ref, window_ref, response_ref, mixed_ref, total_ref, copy_sems):
    kind = pl.program_id(0)
    kinds = pl.num_programs(0)
    input_rows, cols, _ = local_ref.shape
    output_rows = input_rows + 2 * RIM
    parts = (far_west_ref, west_ref, local_ref, east_ref, far_east_ref)

    @pl.when(kind == 0)
    def _():
        copies = [
            pltpu.make_async_copy(part, window_ref.at[:, index * cols : (index + 1) * cols, :], copy_sems.at[index])
            for index, part in enumerate(parts)
        ]
        for copy in copies:
            copy.start()
        for copy in copies:
            copy.wait()

    for in_row in range(input_rows):
        response = jnp.dot(band_ref[in_row, 0], window_ref[in_row], preferred_element_type=jnp.float32)
        response_ref[in_row * cols : (in_row + 1) * cols, :] = response.astype(jnp.bfloat16)
    mixed_ref[...] = jnp.dot(response_ref[...], weight_ref[0], preferred_element_type=jnp.float32)
    chunk = 16

    def accumulate(first):
        def body(step, carry):
            start = pl.multiple_of(step * chunk, chunk)
            pieces = [mixed_ref[pl.ds(in_row * cols + start, chunk), :] for in_row in range(input_rows)]
            for out_row in range(output_rows):
                total = None if first else total_ref[out_row, pl.ds(start, chunk), :]
                for in_row in range(max(0, out_row - 2 * RIM), min(input_rows, out_row + 1)):
                    scale = counts_ref[(out_row * kinds + kind) * input_rows + in_row]
                    term = scale * pieces[in_row]
                    total = term if total is None else total + term
                total_ref[out_row, pl.ds(start, chunk), :] = total
            return carry

        lax.fori_loop(0, cols // chunk, body, 0)

    pl.when(kind == 0)(lambda: accumulate(True))
    pl.when(kind > 0)(lambda: accumulate(False))

    @pl.when(kind == kinds - 1)
    def _():
        inner_ref[...] = total_ref[RIM : RIM + input_rows]
        upper_ref[...] = total_ref[:RIM].astype(upper_ref.dtype)
        lower_ref[...] = total_ref[RIM + input_rows :].astype(lower_ref.dtype)


def block_partials(counts, short_taps, parts, mix_weight):
    rows, cols, channels = parts[0].shape
    kinds = short_taps.shape[1]
    window = cols * len(parts)
    band = band_matrix(short_taps, cols, window)
    whole = lambda shape: pl.BlockSpec(shape, lambda k: (0,) * len(shape))
    return pl.pallas_call(
        _block_kernel,
        grid=(kinds,),
        in_specs=[
            pl.BlockSpec(memory_space=pltpu.SMEM),
            pl.BlockSpec((rows, 1, cols, window), lambda k: (0, k, 0, 0)),
        ]
        + [pl.BlockSpec(memory_space=pl.ANY)] * len(parts)
        + [pl.BlockSpec((1,) + mix_weight.shape[1:], lambda k: (k, 0, 0))],
        out_specs=[whole((RIM, cols, channels))] * 2 + [whole((rows, cols, channels))],
        out_shape=[
            jax.ShapeDtypeStruct((RIM, cols, channels), jnp.bfloat16),
            jax.ShapeDtypeStruct((RIM, cols, channels), jnp.bfloat16),
            jax.ShapeDtypeStruct((rows, cols, channels), jnp.float32),
        ],
        scratch_shapes=[
            pltpu.VMEM((rows, window, channels), jnp.bfloat16),
            pltpu.VMEM((rows * cols, channels), jnp.bfloat16),
            pltpu.VMEM((rows * cols, mix_weight.shape[2]), jnp.float32),
            pltpu.VMEM((rows + 2 * RIM, cols, mix_weight.shape[2]), jnp.float32),
            pltpu.SemaphoreType.DMA((len(parts),)),
        ],
        compiler_params=pltpu.CompilerParams(dimension_semantics=("arbitrary",)),
    )(counts.reshape(-1), band, *parts, mix_weight)


def on_device(field, lon_width, lon_taps, row_scale, support, mix_weight):
    rows = field.shape[0]
    kinds = lon_taps.shape[1]
    far_west, west, east, far_east = longitude_halo(field)
    short_taps = masked_taps(lon_taps, lon_width)
    entries = support.shape[0]
    lists = with_halo(support, (("lat", 0),), entries)
    above = lists[:entries]
    below = lists[2 * entries :]
    out_rows = jnp.concatenate(
        [support[:, 0] + RIM, above[:, 0] - rows + RIM, below[:, 0] + rows + RIM]
    )
    in_rows = jnp.concatenate([support[:, 1], above[:, 1] - rows, below[:, 1] + rows])
    basis = jnp.concatenate([support[:, 2], above[:, 2], below[:, 2]])
    valid = jnp.concatenate(
        [(support[:, 1] >= 0) & (support[:, 1] < rows), above[:, 1] >= rows, below[:, 1] < 0]
    )
    counts = coupling(out_rows, in_rows, basis, valid, rows + 2 * RIM, rows, kinds)
    upper, lower, inner = block_partials(
        counts, short_taps, (far_west, west, field, east, far_east), mix_weight
    )
    count = lax.axis_size("lat")
    forward = [(i, i + 1) for i in range(count - 1)]
    backward = [(target, source) for source, target in forward]
    from_below = lax.ppermute(upper, "lat", backward).astype(jnp.float32)
    from_above = lax.ppermute(lower, "lat", forward).astype(jnp.float32)
    inner = inner + jnp.pad(from_above, ((0, rows - RIM), (0, 0), (0, 0)))
    inner = inner + jnp.pad(from_below, ((rows - RIM, 0), (0, 0), (0, 0)))
    return (inner * row_scale[:, None, None]).astype(jnp.bfloat16)


def solution(mesh):
    in_specs = (
        P("lat", "lon", None),
        P("lat"),
        P("lat", None, None),
        P("lat"),
        P("lat", None),
        P(),
    )
    out_specs = P("lat", "lon", None)
    return jax.shard_map(
        on_device, mesh=mesh, in_specs=in_specs, out_specs=out_specs, check_vma=False
    )
```
